128 devices in a mesh: mode: 8 (over y, z_lo), depth: 16 (over x, z_hi, core).
Axes of the slice: x: 4, y: 4, z: 4 (z_hi: 2, z_lo: 2; z = z_hi * 2 + z_lo), core: 2. Of those that a mesh axis runs over, the one named last changes fastest.
Arguments:
- fields: float32 [40, 512, 16, 128], P('mode', 'depth'), may hold values from -6 to 6
- mean_field: float32 [512, 16, 128], P('depth'), may hold values from 0.5 to 2
- kl_modes: float32 [7, 512, 16, 128], P(None, 'depth'), may hold values from -3 to 3
- decay: float32 [512, 16, 128], P('depth'), may hold values from 0.4 to 1, as said below
- coupling: float32 [40, 40, 8], replicated, may hold values from -0.09375 to 0.09375
- pattern: int32 [40, 40, 8], replicated, may hold values 0 or 1
- mode_order: int32 [40], replicated, may hold values from 0 to 39, each once
Outputs:
- preconditioned: float32 [40, 512, 16, 128], P('mode', 'depth')
The draws below stay inside these ranges and needn't reach their ends.
Inputs may be any that keep to these rules, and one draw needn't show every extreme that they name: decay lies strictly between 0 and 1 in every cell. mode_order names each of the 40 modes once.
All inputs are finite; a program needn't handle non-finite values.
Results may differ from the reference program's by a relative error of at most 0.0003.
Values sent between devices are 32-bit elements; how exact they have to be, the bound alone decides.
No kernel may reach another device: no remote copies, remote signals or barrier semaphores. Data moves between devices by JAX's collectives and lax.ppermute only.
A program may use at most 128 MiB of HBM per device.

```python
import math
import jax
import jax.numpy as jnp
from jax import lax

MODES = 40
KL = 7
KT = 8
LX = 16
LY = 128
DEPTH_CELLS = 512


def draw_decay(key, part):
    child_random_keys = jax.random.split(jax.random.fold_in(key, 11), 6)
    column_profile = (1, LX, LY)
    slow_share = 0.5
    chooser = jax.random.uniform(child_random_keys[0], column_profile)
    slow_rate = jnp.exp(jax.random.uniform(child_random_keys[1], column_profile, minval=jnp.log(0.1), maxval=jnp.log(0.8))) / DEPTH_CELLS
    fast_rate = jnp.exp(jax.random.uniform(child_random_keys[2], column_profile, minval=jnp.log(1.0 / 50.0), maxval=jnp.log(1.0 / 30.0)))
    falloff_speed = jnp.where(chooser < slow_share, slow_rate, fast_rate)
    surface_jaggedness = jnp.exp(jax.random.uniform(child_random_keys[3], (DEPTH_CELLS, LX, LY), minval=jnp.log(0.5), maxval=jnp.log(2.0)))
    spike_row_list = jax.random.randint(child_random_keys[4], (2,), 0, DEPTH_CELLS)
    spike_retained = jax.random.uniform(child_random_keys[5], column_profile, minval=0.5, maxval=0.8)
    depth_position = jnp.arange(DEPTH_CELLS)[:, None, None]
    spike_selected = (depth_position == spike_row_list[0]) | (depth_position == spike_row_list[1])
    return (jnp.where(spike_selected, spike_retained, 1.0) * jnp.exp(-falloff_speed * surface_jaggedness)).astype(jnp.float32)


def set_ends(entries, rng, low, top_value):
    longest = entries.shape.index(max(entries.shape))
    spots = []
    for shift in (0, 1):
        where = [jax.random.randint(jax.random.fold_in(rng, axis), (), 0, length) for axis, length in enumerate(entries.shape)]
        where[longest] = (where[longest] + shift) % entries.shape[longest]
        spots.append(tuple(where))
    return entries.at[spots[0]].set(low).at[spots[1]].set(top_value)


def level_of(rng, dims, shards, low, largest):
    loudness = 1.0
    for position, shards_of in shards:
        steps = jax.random.uniform(jax.random.fold_in(jax.random.fold_in(rng, 6), position), (shards_of,), jnp.float32, low / len(shards), largest / len(shards))
        loudness = loudness * jnp.repeat(jnp.exp(steps), dims[position] // shards_of).reshape((-1,) + (1,) * (len(dims) - 1 - position))
    return loudness


def noise(key, shape, spread, most, shards=(), kind=jnp.bfloat16):
    factor_of = level_of(key, shape, shards, -0.22, 0.18) if shards else 1.0
    array = jax.random.normal(key, shape, jnp.float32) * spread * factor_of
    return jnp.minimum(jnp.maximum(array, -most), most).astype(kind)


def setup_inputs(seed: int = 0) -> dict:
    arg_keys = jax.random.split(jax.random.key(seed), 8)
    fields = noise(arg_keys[0], (MODES, DEPTH_CELLS, LX, LY), 1.0, 6.0, ((0, 8), (1, 16)), jnp.float32)
    mean_field = jnp.clip(jnp.exp(math.log(2.0) - 1.3862944 * jax.random.uniform(arg_keys[1], (DEPTH_CELLS, LX, LY), jnp.float32) ** level_of(arg_keys[1], (DEPTH_CELLS, LX, LY), ((0, 16),), -0.2, 0.2)), 0.5, 2.0)
    kl_modes = noise(arg_keys[2], (KL, DEPTH_CELLS, LX, LY), 0.5, 3.0, ((1, 16),), jnp.float32)
    decay = draw_decay(jax.random.fold_in(arg_keys[7], 71), 0)
    coupling = noise(arg_keys[4], (MODES, MODES, KT), (14 * MODES * KT) ** -0.5, 0.09375, (), jnp.float32)
    pattern = set_ends((jax.random.randint(arg_keys[5], (MODES, MODES, KT), 0, 3) < 1).astype(jnp.int32), jax.random.fold_in(arg_keys[5], 1), 0, 1)
    mode_order = jax.random.permutation(arg_keys[6], MODES).astype(jnp.int32)
    return dict(fields=fields, mean_field=mean_field, kl_modes=kl_modes, decay=decay, coupling=coupling, pattern=pattern, mode_order=mode_order)


def laplace(field):
    lateral = jnp.pad(field, ((0, 0), (1, 1), (1, 1), (1, 1)))
    centre = lateral[:, 1:-1, 1:-1, 1:-1]
    beside = lateral[:, 2:, 1:-1, 1:-1] + lateral[:, :-2, 1:-1, 1:-1]
    beside = beside + lateral[:, 1:-1, 2:, 1:-1] + lateral[:, 1:-1, :-2, 1:-1]
    beside = beside + lateral[:, 1:-1, 1:-1, 2:] + lateral[:, 1:-1, 1:-1, :-2]
    return 6.0 * centre - beside

def recurrence(ratio_field, source):

    def advance(carried, inputs):
        ratio_row, source_row = inputs
        carried = ratio_row * carried + source_row
        return (carried, carried)
    initial = jnp.zeros((source.shape[0],) + source.shape[2:], source.dtype)
    final_state, states = lax.scan(advance, initial, (ratio_field, jnp.moveaxis(source, 1, 0)))
    return jnp.moveaxis(states, 0, 1)

def reference(fields, mean_field, kl_modes, decay, coupling, pattern, mode_order):
    masked = coupling * pattern.astype(coupling.dtype)
    coupling_table = masked[mode_order][:, mode_order]
    stencil_out = laplace(fields)
    flattened = stencil_out.reshape(MODES, -1)
    coefficients = jnp.concatenate([mean_field[None], kl_modes], axis=0).reshape(KT, -1)
    mixed_field = jnp.zeros_like(flattened)
    for term_index in range(KT):
        mixed_field = mixed_field + coefficients[term_index] * jnp.dot(coupling_table[:, :, term_index], flattened, precision=lax.Precision.HIGHEST)
    mixed_field = mixed_field.reshape(fields.shape)
    gain_field = jnp.sqrt(1.0 - decay * decay)
    smooth = recurrence(decay, gain_field[None] * mixed_field)
    backward = recurrence(jnp.flip(decay, axis=0), jnp.flip(gain_field[None] * smooth, axis=1))
    return jnp.flip(backward, axis=1)
```

```python
import jax
import jax.numpy as jnp
from jax import lax
from jax.experimental import pallas as pl
from jax.experimental.pallas import tpu as pltpu
from jax.sharding import PartitionSpec as P


def with_halo(cells, sides, width):
    for axis, dim in sides:
        count = lax.axis_size(axis)
        ends = count - 1
        head = lax.slice_in_dim(cells, 0, width, axis=dim)
        tail = lax.slice_in_dim(cells, cells.shape[dim] - width, cells.shape[dim], axis=dim)
        cells = jnp.concatenate(
            [
                lax.ppermute(tail, axis, [(i, (i + 1) % count) for i in range(ends)]),
                cells,
                lax.ppermute(head, axis, [((i + 1) % count, i) for i in range(ends)]),
            ],
            axis=dim,
        )
    return cells


def laplace(padded):
    lateral = jnp.pad(padded, ((0, 0), (0, 0), (1, 1), (1, 1)))
    centre = lateral[:, 1:-1, 1:-1, 1:-1]
    beside = lateral[:, 2:, 1:-1, 1:-1] + lateral[:, :-2, 1:-1, 1:-1]
    beside = beside + lateral[:, 1:-1, 2:, 1:-1] + lateral[:, 1:-1, :-2, 1:-1]
    beside = beside + lateral[:, 1:-1, 1:-1, 2:] + lateral[:, 1:-1, 1:-1, :-2]
    return 6.0 * centre - beside


def sweep_kernel(mixed_ref, decay_ref, back_ref, coupled_ref, tail_ref, forward_ref):
    rows = decay_ref.shape[0]

    def forward_row(z, carried):
        state, ratio = carried
        d = decay_ref[z]
        g = jnp.sqrt(1.0 - d * d)
        state = d[None] * state + g[None] * mixed_ref[:, z]
        ratio = d * ratio
        back_ref[:, z] = g[None] * state
        coupled_ref[z] = g * ratio
        return state, ratio

    lateral = decay_ref.shape[1:]
    modes = mixed_ref.shape[0]
    state, _ = lax.fori_loop(
        0,
        rows,
        forward_row,
        (jnp.zeros((modes,) + lateral, jnp.float32), jnp.ones(lateral, jnp.float32)),
    )
    forward_ref[...] = state

    def backward_row(i, carried):
        z = rows - 1 - i
        back, coupled, tail = carried
        d = decay_ref[z]
        back = d[None] * back + back_ref[:, z]
        coupled = d * coupled + coupled_ref[z]
        tail = d * tail
        back_ref[:, z] = back
        coupled_ref[z] = coupled
        tail_ref[z] = tail
        return back, coupled, tail

    lax.fori_loop(
        0,
        rows,
        backward_row,
        (
            jnp.zeros((modes,) + lateral, jnp.float32),
            jnp.zeros(lateral, jnp.float32),
            jnp.ones(lateral, jnp.float32),
        ),
    )


def local_sweeps(mixed, decay):
    modes, rows = mixed.shape[0], mixed.shape[1]
    lateral = mixed.shape[2:]
    return pl.pallas_call(
        sweep_kernel,
        out_shape=(
            jax.ShapeDtypeStruct(mixed.shape, jnp.float32),
            jax.ShapeDtypeStruct(decay.shape, jnp.float32),
            jax.ShapeDtypeStruct(decay.shape, jnp.float32),
            jax.ShapeDtypeStruct((modes,) + lateral, jnp.float32),
        ),
    )(mixed, decay)


def local(fields, mean_field, kl_modes, decay, coupling, pattern, mode_order):
    local_modes = fields.shape[0]
    rows = fields.shape[1]
    lateral = fields.shape[2:]
    mode_total = mode_order.shape[0]
    groups = lax.axis_size("mode")
    chunk = rows // groups
    masked = coupling * pattern.astype(jnp.float32)
    coupling_table = jnp.take(jnp.take(masked, mode_order, axis=0), mode_order, axis=1)
    term_total = coupling_table.shape[2]

    padded = with_halo(fields, (("depth", 1),), 1)
    stencil = laplace(padded)
    stencil_rows = lax.all_to_all(stencil, "mode", 1, 0, tiled=True)
    cell_count = chunk * lateral[0] * lateral[1]
    stencil_rows = stencil_rows.reshape(mode_total, cell_count)

    coefficients = jnp.concatenate([mean_field[None], kl_modes], axis=0)
    my_chunk = lax.axis_index("mode") * chunk
    coefficients = lax.dynamic_slice_in_dim(coefficients, my_chunk, chunk, axis=1)
    coefficients = coefficients.reshape(term_total, 1, cell_count)

    table_rows = jnp.transpose(coupling_table, (2, 0, 1)).reshape(term_total * mode_total, mode_total)
    accumulated = jnp.dot(
        table_rows,
        stencil_rows,
        precision=lax.Precision.HIGHEST,
        preferred_element_type=jnp.float32,
    ).reshape(term_total, mode_total, cell_count)
    mixed_rows = jnp.sum(coefficients * accumulated, axis=0)
    mixed_rows = mixed_rows.reshape((mode_total, chunk) + lateral)
    mixed_field = lax.all_to_all(mixed_rows, "mode", 0, 1, tiled=True)

    back, coupled, tail, forward_end = local_sweeps(mixed_field, decay)
    summary = jnp.concatenate(
        [tail[:1], coupled[:1], forward_end, back[:, 0]], axis=0
    )
    summaries = lax.all_gather(summary, "depth", axis=0, tiled=False)
    slabs = summaries.shape[0]
    ratio_all = summaries[:, 0]
    coupled_all = summaries[:, 1]
    forward_all = summaries[:, 2 : 2 + local_modes]
    back_all = summaries[:, 2 + local_modes :]

    state_low = [jnp.zeros_like(forward_all[0])]
    for slab in range(slabs - 1):
        state_low.append(ratio_all[slab][None] * state_low[-1] + forward_all[slab])
    state_high = [jnp.zeros_like(forward_all[0])]
    for slab in range(slabs - 1, 0, -1):
        state_high.append(
            back_all[slab]
            + coupled_all[slab][None] * state_low[slab]
            + ratio_all[slab][None] * state_high[-1]
        )
    state_high = state_high[::-1]
    me = lax.axis_index("depth")
    low = lax.dynamic_index_in_dim(jnp.stack(state_low), me, 0, keepdims=False)
    high = lax.dynamic_index_in_dim(jnp.stack(state_high), me, 0, keepdims=False)
    return back + coupled[None] * low[:, None] + tail[None] * high[:, None]


def solution(mesh):
    in_specs = (
        P("mode", "depth", None, None),
        P("depth", None, None),
        P(None, "depth", None, None),
        P("depth", None, None),
        P(),
        P(),
        P(),
    )
    out_specs = P("mode", "depth", None, None)
    return jax.shard_map(local, mesh=mesh, in_specs=in_specs, out_specs=out_specs, check_vma=False)
```

```python
import jax
import jax.numpy as jnp
from jax import lax
from jax.experimental import pallas as pl
from jax.experimental.pallas import tpu as pltpu
from jax.sharding import PartitionSpec as P


def with_halo(cells, sides, width):
    for axis, dim in sides:
        count = lax.axis_size(axis)
        ends = count - 1
        head = lax.slice_in_dim(cells, 0, width, axis=dim)
        tail = lax.slice_in_dim(cells, cells.shape[dim] - width, cells.shape[dim], axis=dim)
        cells = jnp.concatenate(
            [
                lax.ppermute(tail, axis, [(i, (i + 1) % count) for i in range(ends)]),
                cells,
                lax.ppermute(head, axis, [((i + 1) % count, i) for i in range(ends)]),
            ],
            axis=dim,
        )
    return cells


def laplace(padded):
    lateral = jnp.pad(padded, ((0, 0), (0, 0), (1, 1), (1, 1)))
    centre = lateral[:, 1:-1, 1:-1, 1:-1]
    beside = lateral[:, 2:, 1:-1, 1:-1] + lateral[:, :-2, 1:-1, 1:-1]
    beside = beside + lateral[:, 1:-1, 2:, 1:-1] + lateral[:, 1:-1, :-2, 1:-1]
    beside = beside + lateral[:, 1:-1, 1:-1, 2:] + lateral[:, 1:-1, 1:-1, :-2]
    return 6.0 * centre - beside


def sweep_kernel(mixed_ref, decay_ref, back_ref, coupled_ref, tail_ref, forward_ref):
    rows = decay_ref.shape[0]

    def forward_row(z, carried):
        state, ratio = carried
        d = decay_ref[z]
        g = jnp.sqrt(1.0 - d * d)
        state = d[None] * state + g[None] * mixed_ref[:, z]
        ratio = d * ratio
        back_ref[:, z] = g[None] * state
        coupled_ref[z] = g * ratio
        return state, ratio

    lateral = decay_ref.shape[1:]
    modes = mixed_ref.shape[0]
    state, _ = lax.fori_loop(
        0,
        rows,
        forward_row,
        (jnp.zeros((modes,) + lateral, jnp.float32), jnp.ones(lateral, jnp.float32)),
    )
    forward_ref[...] = state

    def backward_row(i, carried):
        z = rows - 1 - i
        back, coupled, tail = carried
        d = decay_ref[z]
        back = d[None] * back + back_ref[:, z]
        coupled = d * coupled + coupled_ref[z]
        tail = d * tail
        back_ref[:, z] = back
        coupled_ref[z] = coupled
        tail_ref[z] = tail
        return back, coupled, tail

    lax.fori_loop(
        0,
        rows,
        backward_row,
        (
            jnp.zeros((modes,) + lateral, jnp.float32),
            jnp.zeros(lateral, jnp.float32),
            jnp.ones(lateral, jnp.float32),
        ),
    )


def local_sweeps(mixed, decay):
    modes, rows = mixed.shape[0], mixed.shape[1]
    lateral = mixed.shape[2:]
    return pl.pallas_call(
        sweep_kernel,
        out_shape=(
            jax.ShapeDtypeStruct(mixed.shape, jnp.float32),
            jax.ShapeDtypeStruct(decay.shape, jnp.float32),
            jax.ShapeDtypeStruct(decay.shape, jnp.float32),
            jax.ShapeDtypeStruct((modes,) + lateral, jnp.float32),
        ),
    )(mixed, decay)


def local(fields, mean_field, kl_modes, decay, coupling, pattern, mode_order):
    local_modes = fields.shape[0]
    rows = fields.shape[1]
    lateral = fields.shape[2:]
    mode_total = mode_order.shape[0]
    groups = lax.axis_size("mode")
    chunk = rows // groups
    masked = coupling * pattern.astype(jnp.float32)
    coupling_table = jnp.take(jnp.take(masked, mode_order, axis=0), mode_order, axis=1)
    term_total = coupling_table.shape[2]

    padded = with_halo(fields, (("depth", 1),), 1)
    stencil = laplace(padded)
    stencil_rows = lax.all_to_all(stencil, "mode", 1, 0, tiled=True)
    cell_count = chunk * lateral[0] * lateral[1]
    stencil_rows = stencil_rows.reshape(mode_total, cell_count)

    coefficients = jnp.concatenate([mean_field[None], kl_modes], axis=0)
    my_chunk = lax.axis_index("mode") * chunk
    coefficients = lax.dynamic_slice_in_dim(coefficients, my_chunk, chunk, axis=1)
    coefficients = coefficients.reshape(term_total, 1, cell_count)

    table_rows = jnp.transpose(coupling_table, (2, 0, 1)).reshape(term_total * mode_total, mode_total)
    accumulated = jnp.dot(
        table_rows,
        stencil_rows,
        precision=lax.Precision.HIGHEST,
        preferred_element_type=jnp.float32,
    ).reshape(term_total, mode_total, cell_count)
    mixed_rows = jnp.sum(coefficients * accumulated, axis=0)
    mixed_rows = mixed_rows.reshape((mode_total, chunk) + lateral)
    mixed_field = lax.all_to_all(mixed_rows, "mode", 0, 1, tiled=True)

    back, coupled, tail, forward_end = local_sweeps(mixed_field, decay)
    summary = jnp.concatenate(
        [tail[:1], coupled[:1], forward_end, back[:, 0]], axis=0
    )
    slabs = lax.axis_size("depth")
    copies = jnp.broadcast_to(summary[None], (slabs,) + summary.shape)
    summaries = lax.all_to_all(copies, "depth", 0, 0, tiled=True)
    ratio_all = summaries[:, 0]
    coupled_all = summaries[:, 1]
    forward_all = summaries[:, 2 : 2 + local_modes]
    back_all = summaries[:, 2 + local_modes :]

    state_low = [jnp.zeros_like(forward_all[0])]
    for slab in range(slabs - 1):
        state_low.append(ratio_all[slab][None] * state_low[-1] + forward_all[slab])
    state_high = [jnp.zeros_like(forward_all[0])]
    for slab in range(slabs - 1, 0, -1):
        state_high.append(
            back_all[slab]
            + coupled_all[slab][None] * state_low[slab]
            + ratio_all[slab][None] * state_high[-1]
        )
    state_high = state_high[::-1]
    me = lax.axis_index("depth")
    low = lax.dynamic_index_in_dim(jnp.stack(state_low), me, 0, keepdims=False)
    high = lax.dynamic_index_in_dim(jnp.stack(state_high), me, 0, keepdims=False)
    return back + coupled[None] * low[:, None] + tail[None] * high[:, None]


def solution(mesh):
    in_specs = (
        P("mode", "depth", None, None),
        P("depth", None, None),
        P(None, "depth", None, None),
        P("depth", None, None),
        P(),
        P(),
        P(),
    )
    out_specs = P("mode", "depth", None, None)
    return jax.shard_map(local, mesh=mesh, in_specs=in_specs, out_specs=out_specs, check_vma=False)
```

```python
import jax
import jax.numpy as jnp
from jax import lax
from jax.experimental import pallas as pl
from jax.experimental.pallas import tpu as pltpu
from jax.sharding import PartitionSpec as P


def with_halo(cells, sides, width):
    for axis, dim in sides:
        count = lax.axis_size(axis)
        ends = count - 1
        head = lax.slice_in_dim(cells, 0, width, axis=dim)
        tail = lax.slice_in_dim(cells, cells.shape[dim] - width, cells.shape[dim], axis=dim)
        cells = jnp.concatenate(
            [
                lax.ppermute(tail, axis, [(i, (i + 1) % count) for i in range(ends)]),
                cells,
                lax.ppermute(head, axis, [((i + 1) % count, i) for i in range(ends)]),
            ],
            axis=dim,
        )
    return cells


def laplace(padded):
    lateral = jnp.pad(padded, ((0, 0), (0, 0), (1, 1), (1, 1)))
    centre = lateral[:, 1:-1, 1:-1, 1:-1]
    beside = lateral[:, 2:, 1:-1, 1:-1] + lateral[:, :-2, 1:-1, 1:-1]
    beside = beside + lateral[:, 1:-1, 2:, 1:-1] + lateral[:, 1:-1, :-2, 1:-1]
    beside = beside + lateral[:, 1:-1, 1:-1, 2:] + lateral[:, 1:-1, 1:-1, :-2]
    return 6.0 * centre - beside


def sweep_kernel(mixed_ref, decay_ref, back_ref, coupled_ref, tail_ref, summary_ref):
    rows = decay_ref.shape[0]

    def forward_row(z, carried):
        state, ratio = carried
        d = decay_ref[z]
        g = jnp.sqrt(1.0 - d * d)
        state = d[None] * state + g[None] * mixed_ref[:, z]
        ratio = d * ratio
        back_ref[:, z] = g[None] * state
        coupled_ref[z] = g * ratio
        return state, ratio

    lateral = decay_ref.shape[1:]
    modes = mixed_ref.shape[0]
    state, _ = lax.fori_loop(
        0,
        rows,
        forward_row,
        (jnp.zeros((modes,) + lateral, jnp.float32), jnp.ones(lateral, jnp.float32)),
    )

    def backward_row(i, carried):
        z = rows - 1 - i
        back, coupled, tail = carried
        d = decay_ref[z]
        back = d[None] * back + back_ref[:, z]
        coupled = d * coupled + coupled_ref[z]
        tail = d * tail
        back_ref[:, z] = back
        coupled_ref[z] = coupled
        tail_ref[z] = tail
        return back, coupled, tail

    back, coupled, tail = lax.fori_loop(
        0,
        rows,
        backward_row,
        (
            jnp.zeros((modes,) + lateral, jnp.float32),
            jnp.zeros(lateral, jnp.float32),
            jnp.ones(lateral, jnp.float32),
        ),
    )
    for copy in range(summary_ref.shape[0]):
        summary_ref[copy, 0] = tail
        summary_ref[copy, 1] = coupled
        summary_ref[copy, 2 : 2 + modes] = state
        summary_ref[copy, 2 + modes :] = back


def local_sweeps(mixed, decay, copies):
    modes, rows = mixed.shape[0], mixed.shape[1]
    lateral = mixed.shape[2:]
    return pl.pallas_call(
        sweep_kernel,
        out_shape=(
            jax.ShapeDtypeStruct(mixed.shape, jnp.float32),
            jax.ShapeDtypeStruct(decay.shape, jnp.float32),
            jax.ShapeDtypeStruct(decay.shape, jnp.float32),
            jax.ShapeDtypeStruct((copies, 2 + 2 * modes) + lateral, jnp.float32),
        ),
    )(mixed, decay)


def local(fields, mean_field, kl_modes, decay, coupling, pattern, mode_order):
    local_modes = fields.shape[0]
    rows = fields.shape[1]
    lateral = fields.shape[2:]
    mode_total = mode_order.shape[0]
    groups = lax.axis_size("mode")
    chunk = rows // groups
    masked = coupling * pattern.astype(jnp.float32)
    coupling_table = jnp.take(jnp.take(masked, mode_order, axis=0), mode_order, axis=1)
    term_total = coupling_table.shape[2]

    padded = with_halo(fields, (("depth", 1),), 1)
    stencil = laplace(padded)
    stencil_rows = lax.all_to_all(stencil, "mode", 1, 0, tiled=True)
    cell_count = chunk * lateral[0] * lateral[1]
    stencil_rows = stencil_rows.reshape(mode_total, cell_count)

    coefficients = jnp.concatenate([mean_field[None], kl_modes], axis=0)
    my_chunk = lax.axis_index("mode") * chunk
    coefficients = lax.dynamic_slice_in_dim(coefficients, my_chunk, chunk, axis=1)
    coefficients = coefficients.reshape(term_total, 1, cell_count)

    table_rows = jnp.transpose(coupling_table, (2, 0, 1)).reshape(term_total * mode_total, mode_total)
    accumulated = jnp.dot(
        table_rows,
        stencil_rows,
        precision=lax.Precision.HIGHEST,
        preferred_element_type=jnp.float32,
    ).reshape(term_total, mode_total, cell_count)
    mixed_rows = jnp.sum(coefficients * accumulated, axis=0)
    mixed_rows = mixed_rows.reshape((mode_total, chunk) + lateral)
    mixed_field = lax.all_to_all(mixed_rows, "mode", 0, 1, tiled=True)

    slabs = lax.axis_size("depth")
    back, coupled, tail, copies = local_sweeps(mixed_field, decay, slabs)
    summaries = lax.all_to_all(copies, "depth", 0, 0, tiled=True)
    ratio_all = summaries[:, 0]
    coupled_all = summaries[:, 1]
    forward_all = summaries[:, 2 : 2 + local_modes]
    back_all = summaries[:, 2 + local_modes :]

    me = lax.axis_index("depth")
    entering = [jnp.zeros_like(forward_all[0])]
    for slab in range(slabs - 1):
        entering.append(ratio_all[slab][None] * entering[-1] + forward_all[slab])
    low = entering[0]
    for slab in range(1, slabs):
        low = jnp.where(me == slab, entering[slab], low)
    above = jnp.zeros_like(forward_all[0])
    high = above
    for slab in range(slabs - 1, 0, -1):
        above = (
            back_all[slab]
            + coupled_all[slab][None] * entering[slab]
            + ratio_all[slab][None] * above
        )
        high = jnp.where(me == slab - 1, above, high)
    return back + coupled[None] * low[:, None] + tail[None] * high[:, None]


def solution(mesh):
    in_specs = (
        P("mode", "depth", None, None),
        P("depth", None, None),
        P(None, "depth", None, None),
        P("depth", None, None),
        P(),
        P(),
        P(),
    )
    out_specs = P("mode", "depth", None, None)
    return jax.shard_map(local, mesh=mesh, in_specs=in_specs, out_specs=out_specs, check_vma=False)
```

```python
import jax
import jax.numpy as jnp
from jax import lax
from jax.experimental import pallas as pl
from jax.experimental.pallas import tpu as pltpu
from jax.sharding import PartitionSpec as P


def with_halo(cells, sides, width):
    for axis, dim in sides:
        count = lax.axis_size(axis)
        ends = count - 1
        head = lax.slice_in_dim(cells, 0, width, axis=dim)
        tail = lax.slice_in_dim(cells, cells.shape[dim] - width, cells.shape[dim], axis=dim)
        cells = jnp.concatenate(
            [
                lax.ppermute(tail, axis, [(i, (i + 1) % count) for i in range(ends)]),
                cells,
                lax.ppermute(head, axis, [((i + 1) % count, i) for i in range(ends)]),
            ],
            axis=dim,
        )
    return cells


def laplace(padded):
    lateral = jnp.pad(padded, ((0, 0), (0, 0), (1, 1), (1, 1)))
    centre = lateral[:, 1:-1, 1:-1, 1:-1]
    beside = lateral[:, 2:, 1:-1, 1:-1] + lateral[:, :-2, 1:-1, 1:-1]
    beside = beside + lateral[:, 1:-1, 2:, 1:-1] + lateral[:, 1:-1, :-2, 1:-1]
    beside = beside + lateral[:, 1:-1, 1:-1, 2:] + lateral[:, 1:-1, 1:-1, :-2]
    return 6.0 * centre - beside


def sweep_kernel(mixed_ref, decay_ref, back_ref, coupled_ref, tail_ref, summary_ref):
    rows = decay_ref.shape[0]

    def forward_row(z, carried):
        state, ratio = carried
        d = decay_ref[z]
        g = jnp.sqrt(1.0 - d * d)
        state = d[None] * state + g[None] * mixed_ref[:, z]
        ratio = d * ratio
        back_ref[:, z] = g[None] * state
        coupled_ref[z] = g * ratio
        return state, ratio

    lateral = decay_ref.shape[1:]
    modes = mixed_ref.shape[0]
    state, _ = lax.fori_loop(
        0,
        rows,
        forward_row,
        (jnp.zeros((modes,) + lateral, jnp.float32), jnp.ones(lateral, jnp.float32)),
    )

    def backward_row(i, carried):
        z = rows - 1 - i
        back, coupled, tail = carried
        d = decay_ref[z]
        back = d[None] * back + back_ref[:, z]
        coupled = d * coupled + coupled_ref[z]
        tail = d * tail
        back_ref[:, z] = back
        coupled_ref[z] = coupled
        tail_ref[z] = tail
        return back, coupled, tail

    back, coupled, tail = lax.fori_loop(
        0,
        rows,
        backward_row,
        (
            jnp.zeros((modes,) + lateral, jnp.float32),
            jnp.zeros(lateral, jnp.float32),
            jnp.ones(lateral, jnp.float32),
        ),
    )
    for copy in range(summary_ref.shape[0]):
        summary_ref[copy, 0] = tail
        summary_ref[copy, 1] = coupled
        summary_ref[copy, 2 : 2 + modes] = state
        summary_ref[copy, 2 + modes :] = back


def local_sweeps(mixed, decay, copies):
    modes, rows = mixed.shape[0], mixed.shape[1]
    lateral = mixed.shape[2:]
    return pl.pallas_call(
        sweep_kernel,
        out_shape=(
            jax.ShapeDtypeStruct(mixed.shape, jnp.float32),
            jax.ShapeDtypeStruct(decay.shape, jnp.float32),
            jax.ShapeDtypeStruct(decay.shape, jnp.float32),
            jax.ShapeDtypeStruct((copies, 2 + 2 * modes) + lateral, jnp.float32),
        ),
    )(mixed, decay)


def local(fields, mean_field, kl_modes, decay, coupling, pattern, mode_order):
    local_modes = fields.shape[0]
    rows = fields.shape[1]
    lateral = fields.shape[2:]
    mode_total = mode_order.shape[0]
    groups = lax.axis_size("mode")
    chunk = rows // groups
    masked = coupling * pattern.astype(jnp.float32)
    coupling_table = jnp.take(jnp.take(masked, mode_order, axis=0), mode_order, axis=1)
    term_total = coupling_table.shape[2]

    padded = with_halo(fields, (("depth", 1),), 1)
    stencil = laplace(padded)
    stencil_rows = lax.all_to_all(stencil, "mode", 1, 0, tiled=True)
    cell_count = chunk * lateral[0] * lateral[1]
    stencil_rows = stencil_rows.reshape(mode_total, cell_count)

    coefficients = jnp.concatenate([mean_field[None], kl_modes], axis=0)
    my_chunk = lax.axis_index("mode") * chunk
    coefficients = lax.dynamic_slice_in_dim(coefficients, my_chunk, chunk, axis=1)
    coefficients = coefficients.reshape(1, term_total, cell_count)
    weighted = (stencil_rows[:, None, :] * coefficients).reshape(mode_total * term_total, cell_count)
    table_rows = coupling_table.reshape(mode_total, mode_total * term_total)
    mixed_rows = jnp.dot(
        table_rows,
        weighted,
        precision=lax.Precision.HIGH,
        preferred_element_type=jnp.float32,
    )
    mixed_rows = mixed_rows.reshape((mode_total, chunk) + lateral)
    mixed_field = lax.all_to_all(mixed_rows, "mode", 0, 1, tiled=True)

    slabs = lax.axis_size("depth")
    back, coupled, tail, copies = local_sweeps(mixed_field, decay, slabs)
    summaries = lax.all_to_all(copies, "depth", 0, 0, tiled=True)
    ratio_all = summaries[:, 0]
    coupled_all = summaries[:, 1]
    forward_all = summaries[:, 2 : 2 + local_modes]
    back_all = summaries[:, 2 + local_modes :]

    me = lax.axis_index("depth")
    entering = [jnp.zeros_like(forward_all[0])]
    for slab in range(slabs - 1):
        entering.append(ratio_all[slab][None] * entering[-1] + forward_all[slab])
    low = entering[0]
    for slab in range(1, slabs):
        low = jnp.where(me == slab, entering[slab], low)
    above = jnp.zeros_like(forward_all[0])
    high = above
    for slab in range(slabs - 1, 0, -1):
        above = (
            back_all[slab]
            + coupled_all[slab][None] * entering[slab]
            + ratio_all[slab][None] * above
        )
        high = jnp.where(me == slab - 1, above, high)
    return back + coupled[None] * low[:, None] + tail[None] * high[:, None]


def solution(mesh):
    in_specs = (
        P("mode", "depth", None, None),
        P("depth", None, None),
        P(None, "depth", None, None),
        P("depth", None, None),
        P(),
        P(),
        P(),
    )
    out_specs = P("mode", "depth", None, None)
    return jax.shard_map(local, mesh=mesh, in_specs=in_specs, out_specs=out_specs, check_vma=False)
```

```python
import jax
import jax.numpy as jnp
from jax import lax
from jax.experimental import pallas as pl
from jax.experimental.pallas import tpu as pltpu
from jax.sharding import PartitionSpec as P


def with_halo(cells, sides, width):
    for axis, dim in sides:
        count = lax.axis_size(axis)
        ends = count - 1
        head = lax.slice_in_dim(cells, 0, width, axis=dim)
        tail = lax.slice_in_dim(cells, cells.shape[dim] - width, cells.shape[dim], axis=dim)
        cells = jnp.concatenate(
            [
                lax.ppermute(tail, axis, [(i, (i + 1) % count) for i in range(ends)]),
                cells,
                lax.ppermute(head, axis, [((i + 1) % count, i) for i in range(ends)]),
            ],
            axis=dim,
        )
    return cells


def laplace(padded):
    lateral = jnp.pad(padded, ((0, 0), (0, 0), (1, 1), (1, 1)))
    centre = lateral[:, 1:-1, 1:-1, 1:-1]
    beside = lateral[:, 2:, 1:-1, 1:-1] + lateral[:, :-2, 1:-1, 1:-1]
    beside = beside + lateral[:, 1:-1, 2:, 1:-1] + lateral[:, 1:-1, :-2, 1:-1]
    beside = beside + lateral[:, 1:-1, 1:-1, 2:] + lateral[:, 1:-1, 1:-1, :-2]
    return 6.0 * centre - beside


def sweep_kernel(mixed_ref, decay_ref, back_ref, coupled_ref, tail_ref, summary_ref):
    rows = decay_ref.shape[0]

    def forward_row(z, carried):
        state, ratio = carried
        d = decay_ref[z]
        g = jnp.sqrt(1.0 - d * d)
        state = d[None] * state + g[None] * mixed_ref[:, z]
        ratio = d * ratio
        back_ref[:, z] = g[None] * state
        coupled_ref[z] = g * ratio
        return state, ratio

    lateral = decay_ref.shape[1:]
    modes = mixed_ref.shape[0]
    state, _ = lax.fori_loop(
        0,
        rows,
        forward_row,
        (jnp.zeros((modes,) + lateral, jnp.float32), jnp.ones(lateral, jnp.float32)),
    )

    def backward_row(i, carried):
        z = rows - 1 - i
        back, coupled, tail = carried
        d = decay_ref[z]
        back = d[None] * back + back_ref[:, z]
        coupled = d * coupled + coupled_ref[z]
        tail = d * tail
        back_ref[:, z] = back
        coupled_ref[z] = coupled
        tail_ref[z] = tail
        return back, coupled, tail

    back, coupled, tail = lax.fori_loop(
        0,
        rows,
        backward_row,
        (
            jnp.zeros((modes,) + lateral, jnp.float32),
            jnp.zeros(lateral, jnp.float32),
            jnp.ones(lateral, jnp.float32),
        ),
    )
    for copy in range(summary_ref.shape[0]):
        summary_ref[copy, 0] = tail
        summary_ref[copy, 1] = coupled
        summary_ref[copy, 2 : 2 + modes] = state
        summary_ref[copy, 2 + modes :] = back


def local_sweeps(mixed, decay, copies):
    modes, rows = mixed.shape[0], mixed.shape[1]
    lateral = mixed.shape[2:]
    return pl.pallas_call(
        sweep_kernel,
        out_shape=(
            jax.ShapeDtypeStruct(mixed.shape, jnp.float32),
            jax.ShapeDtypeStruct(decay.shape, jnp.float32),
            jax.ShapeDtypeStruct(decay.shape, jnp.float32),
            jax.ShapeDtypeStruct((copies, 2 + 2 * modes) + lateral, jnp.float32),
        ),
    )(mixed, decay)


def local(fields, mean_field, kl_modes, decay, coupling, pattern, mode_order):
    local_modes = fields.shape[0]
    rows = fields.shape[1]
    lateral = fields.shape[2:]
    mode_total = mode_order.shape[0]
    groups = lax.axis_size("mode")
    chunk = rows // groups
    masked = coupling * pattern.astype(jnp.float32)
    coupling_table = jnp.take(jnp.take(masked, mode_order, axis=0), mode_order, axis=1)
    term_total = coupling_table.shape[2]

    padded = with_halo(fields, (("depth", 1),), 1)
    stencil = laplace(padded)
    stencil_rows = lax.all_to_all(stencil, "mode", 1, 0, tiled=True)
    cell_count = chunk * lateral[0] * lateral[1]
    stencil_rows = stencil_rows.reshape(mode_total, cell_count)

    coefficients = jnp.concatenate([mean_field[None], kl_modes], axis=0)
    my_chunk = lax.axis_index("mode") * chunk
    coefficients = lax.dynamic_slice_in_dim(coefficients, my_chunk, chunk, axis=1)
    coefficients = coefficients.reshape(term_total, 1, cell_count)

    table_rows = jnp.transpose(coupling_table, (2, 0, 1)).reshape(term_total * mode_total, mode_total)
    accumulated = jnp.dot(
        table_rows,
        stencil_rows,
        precision=lax.Precision.HIGH,
        preferred_element_type=jnp.float32,
    ).reshape(term_total, mode_total, cell_count)
    mixed_rows = jnp.sum(coefficients * accumulated, axis=0)
    mixed_rows = mixed_rows.reshape((mode_total, chunk) + lateral)
    mixed_field = lax.all_to_all(mixed_rows, "mode", 0, 1, tiled=True)

    slabs = lax.axis_size("depth")
    back, coupled, tail, copies = local_sweeps(mixed_field, decay, slabs)
    summaries = lax.all_to_all(copies, "depth", 0, 0, tiled=True)
    ratio_all = summaries[:, 0]
    coupled_all = summaries[:, 1]
    forward_all = summaries[:, 2 : 2 + local_modes]
    back_all = summaries[:, 2 + local_modes :]

    me = lax.axis_index("depth")
    entering = [jnp.zeros_like(forward_all[0])]
    for slab in range(slabs - 1):
        entering.append(ratio_all[slab][None] * entering[-1] + forward_all[slab])
    low = entering[0]
    for slab in range(1, slabs):
        low = jnp.where(me == slab, entering[slab], low)
    above = jnp.zeros_like(forward_all[0])
    high = above
    for slab in range(slabs - 1, 0, -1):
        above = (
            back_all[slab]
            + coupled_all[slab][None] * entering[slab]
            + ratio_all[slab][None] * above
        )
        high = jnp.where(me == slab - 1, above, high)
    return back + coupled[None] * low[:, None] + tail[None] * high[:, None]


def solution(mesh):
    in_specs = (
        P("mode", "depth", None, None),
        P("depth", None, None),
        P(None, "depth", None, None),
        P("depth", None, None),
        P(),
        P(),
        P(),
    )
    out_specs = P("mode", "depth", None, None)
    return jax.shard_map(local, mesh=mesh, in_specs=in_specs, out_specs=out_specs, check_vma=False)
```

```python
import jax
import jax.numpy as jnp
from jax import lax
from jax.experimental import pallas as pl
from jax.experimental.pallas import tpu as pltpu
from jax.sharding import PartitionSpec as P


def neighbour_sum(x, axis):
    size = x.shape[axis]
    where_from = lax.broadcasted_iota(jnp.int32, x.shape, axis)
    total = jnp.zeros_like(x)
    for shift in (1, size - 1):
        rolled = pltpu.roll(x, shift, axis)
        source = pltpu.roll(where_from, shift, axis)
        inside = jnp.abs(source - where_from) == 1
        total = total + jnp.where(inside, rolled, 0.0)
    return total


def stencil_kernel(fields_ref, out_ref):
    rows = fields_ref.shape[1]

    def one_row(z, carried):
        centre = fields_ref[:, z]
        above = fields_ref[:, jnp.minimum(z + 1, rows - 1)]
        below = fields_ref[:, jnp.maximum(z - 1, 0)]
        beside = jnp.where(z + 1 < rows, above, 0.0) + jnp.where(z > 0, below, 0.0)
        beside = beside + neighbour_sum(centre, 1)
        beside = beside + neighbour_sum(centre, 2)
        out_ref[z] = 6.0 * centre - beside
        return carried

    lax.fori_loop(0, rows, one_row, 0)


def slab_stencil(fields):
    modes, rows = fields.shape[0], fields.shape[1]
    return pl.pallas_call(
        stencil_kernel,
        out_shape=jax.ShapeDtypeStruct((rows, modes) + fields.shape[2:], jnp.float32),
    )(fields)


def sweep_kernel(mixed_ref, decay_ref, back_ref, coupled_ref, tail_ref, summary_ref):
    rows = decay_ref.shape[0]

    def forward_row(z, carried):
        state, ratio = carried
        d = decay_ref[z]
        g = jnp.sqrt(1.0 - d * d)
        state = d[None] * state + g[None] * mixed_ref[:, z]
        ratio = d * ratio
        back_ref[:, z] = g[None] * state
        coupled_ref[z] = g * ratio
        return state, ratio

    lateral = decay_ref.shape[1:]
    modes = mixed_ref.shape[0]
    state, _ = lax.fori_loop(
        0,
        rows,
        forward_row,
        (jnp.zeros((modes,) + lateral, jnp.float32), jnp.ones(lateral, jnp.float32)),
    )

    def backward_row(i, carried):
        z = rows - 1 - i
        back, coupled, tail = carried
        d = decay_ref[z]
        back = d[None] * back + back_ref[:, z]
        coupled = d * coupled + coupled_ref[z]
        tail = d * tail
        back_ref[:, z] = back
        coupled_ref[z] = coupled
        tail_ref[z] = tail
        return back, coupled, tail

    back, coupled, tail = lax.fori_loop(
        0,
        rows,
        backward_row,
        (
            jnp.zeros((modes,) + lateral, jnp.float32),
            jnp.zeros(lateral, jnp.float32),
            jnp.ones(lateral, jnp.float32),
        ),
    )
    for copy in range(summary_ref.shape[0]):
        summary_ref[copy, 0] = tail
        summary_ref[copy, 1] = coupled
        summary_ref[copy, 2 : 2 + modes] = state
        summary_ref[copy, 2 + modes :] = back


def local_sweeps(mixed, decay, copies):
    modes, rows = mixed.shape[0], mixed.shape[1]
    lateral = mixed.shape[2:]
    return pl.pallas_call(
        sweep_kernel,
        out_shape=(
            jax.ShapeDtypeStruct(mixed.shape, jnp.float32),
            jax.ShapeDtypeStruct(decay.shape, jnp.float32),
            jax.ShapeDtypeStruct(decay.shape, jnp.float32),
            jax.ShapeDtypeStruct((copies, 2 + 2 * modes) + lateral, jnp.float32),
        ),
    )(mixed, decay)


def local(fields, mean_field, kl_modes, decay, coupling, pattern, mode_order):
    local_modes = fields.shape[0]
    rows = fields.shape[1]
    lateral = fields.shape[2:]
    mode_total = mode_order.shape[0]
    groups = lax.axis_size("mode")
    chunk = rows // groups
    masked = coupling * pattern.astype(jnp.float32)
    coupling_table = jnp.take(jnp.take(masked, mode_order, axis=0), mode_order, axis=1)
    term_total = coupling_table.shape[2]

    slabs = lax.axis_size("depth")
    from_below = lax.ppermute(fields[:, -1], "depth", [(i, i + 1) for i in range(slabs - 1)])
    from_above = lax.ppermute(fields[:, 0], "depth", [(i + 1, i) for i in range(slabs - 1)])
    stencil = slab_stencil(fields)
    stencil = stencil.at[0].add(-from_below).at[-1].add(-from_above)
    stencil = jnp.transpose(stencil, (1, 0, 2, 3))
    stencil_rows = lax.all_to_all(stencil, "mode", 1, 0, tiled=True)
    cell_count = chunk * lateral[0] * lateral[1]
    stencil_rows = stencil_rows.reshape(mode_total, cell_count)

    coefficients = jnp.concatenate([mean_field[None], kl_modes], axis=0)
    my_chunk = lax.axis_index("mode") * chunk
    coefficients = lax.dynamic_slice_in_dim(coefficients, my_chunk, chunk, axis=1)
    coefficients = coefficients.reshape(term_total, 1, cell_count)

    table_rows = jnp.transpose(coupling_table, (2, 0, 1)).reshape(term_total * mode_total, mode_total)
    accumulated = jnp.dot(
        table_rows,
        stencil_rows,
        precision=lax.Precision.HIGH,
        preferred_element_type=jnp.float32,
    ).reshape(term_total, mode_total, cell_count)
    mixed_rows = jnp.sum(coefficients * accumulated, axis=0)
    mixed_rows = mixed_rows.reshape((mode_total, chunk) + lateral)
    mixed_field = lax.all_to_all(mixed_rows, "mode", 0, 1, tiled=True)

    back, coupled, tail, copies = local_sweeps(mixed_field, decay, slabs)
    summaries = lax.all_to_all(copies, "depth", 0, 0, tiled=True)
    ratio_all = summaries[:, 0]
    coupled_all = summaries[:, 1]
    forward_all = summaries[:, 2 : 2 + local_modes]
    back_all = summaries[:, 2 + local_modes :]

    me = lax.axis_index("depth")
    entering = [jnp.zeros_like(forward_all[0])]
    for slab in range(slabs - 1):
        entering.append(ratio_all[slab][None] * entering[-1] + forward_all[slab])
    low = entering[0]
    for slab in range(1, slabs):
        low = jnp.where(me == slab, entering[slab], low)
    above = jnp.zeros_like(forward_all[0])
    high = above
    for slab in range(slabs - 1, 0, -1):
        above = (
            back_all[slab]
            + coupled_all[slab][None] * entering[slab]
            + ratio_all[slab][None] * above
        )
        high = jnp.where(me == slab - 1, above, high)
    return back + coupled[None] * low[:, None] + tail[None] * high[:, None]


def solution(mesh):
    in_specs = (
        P("mode", "depth", None, None),
        P("depth", None, None),
        P(None, "depth", None, None),
        P("depth", None, None),
        P(),
        P(),
        P(),
    )
    out_specs = P("mode", "depth", None, None)
    return jax.shard_map(local, mesh=mesh, in_specs=in_specs, out_specs=out_specs, check_vma=False)
```

```python
import jax
import jax.numpy as jnp
from jax import lax
from jax.experimental import pallas as pl
from jax.experimental.pallas import tpu as pltpu
from jax.sharding import PartitionSpec as P


def neighbour_masks(shape, axis):
    size = shape[axis]
    where_from = lax.broadcasted_iota(jnp.int32, shape, axis)
    return [
        (shift, jnp.abs(pltpu.roll(where_from, shift, axis) - where_from) == 1)
        for shift in (1, size - 1)
    ]


def stencil_kernel(fields_ref, below_ref, above_ref, out_ref):
    rows = fields_ref.shape[1]
    plane = fields_ref.shape[2:]
    masks = neighbour_masks(plane, 0) + [(s, m) for s, m in neighbour_masks(plane, 1)]
    axes = [0, 0, 1, 1]
    for z in range(rows):
        centre = fields_ref[0, z]
        up = fields_ref[0, z + 1] if z + 1 < rows else above_ref[0]
        down = fields_ref[0, z - 1] if z > 0 else below_ref[0]
        beside = up + down
        for axis, (shift, inside) in zip(axes, masks):
            beside = beside + jnp.where(inside, pltpu.roll(centre, shift, axis), 0.0)
        out_ref[z, 0] = 6.0 * centre - beside


def slab_stencil(fields, below, above):
    modes, rows = fields.shape[0], fields.shape[1]
    plane = fields.shape[2:]
    return pl.pallas_call(
        stencil_kernel,
        grid=(modes,),
        in_specs=[
            pl.BlockSpec((1, rows) + plane, lambda i: (i, 0, 0, 0)),
            pl.BlockSpec((1,) + plane, lambda i: (i, 0, 0)),
            pl.BlockSpec((1,) + plane, lambda i: (i, 0, 0)),
        ],
        out_specs=pl.BlockSpec((rows, 1) + plane, lambda i: (0, i, 0, 0)),
        out_shape=jax.ShapeDtypeStruct((rows, modes) + plane, jnp.float32),
    )(fields, below, above)


def sweep_kernel(mixed_ref, decay_ref, back_ref, coupled_ref, tail_ref, summary_ref):
    rows = decay_ref.shape[0]
    chunk = mixed_ref.shape[2]

    def forward_row(z, carried):
        state, ratio = carried
        d = decay_ref[z]
        g = jnp.sqrt(1.0 - d * d)
        state = d[None] * state + g[None] * mixed_ref[z // chunk, :, z % chunk]
        ratio = d * ratio
        back_ref[:, z] = g[None] * state
        coupled_ref[z] = g * ratio
        return state, ratio

    lateral = decay_ref.shape[1:]
    modes = mixed_ref.shape[1]
    state, _ = lax.fori_loop(
        0,
        rows,
        forward_row,
        (jnp.zeros((modes,) + lateral, jnp.float32), jnp.ones(lateral, jnp.float32)),
    )

    def backward_row(i, carried):
        z = rows - 1 - i
        back, coupled, tail = carried
        d = decay_ref[z]
        back = d[None] * back + back_ref[:, z]
        coupled = d * coupled + coupled_ref[z]
        tail = d * tail
        back_ref[:, z] = back
        coupled_ref[z] = coupled
        tail_ref[z] = tail
        return back, coupled, tail

    back, coupled, tail = lax.fori_loop(
        0,
        rows,
        backward_row,
        (
            jnp.zeros((modes,) + lateral, jnp.float32),
            jnp.zeros(lateral, jnp.float32),
            jnp.ones(lateral, jnp.float32),
        ),
    )
    for copy in range(summary_ref.shape[0]):
        summary_ref[copy, 0] = tail
        summary_ref[copy, 1] = coupled
        summary_ref[copy, 2 : 2 + modes] = state
        summary_ref[copy, 2 + modes :] = back


def local_sweeps(mixed, decay, copies):
    modes = mixed.shape[1]
    rows = decay.shape[0]
    lateral = decay.shape[1:]
    return pl.pallas_call(
        sweep_kernel,
        out_shape=(
            jax.ShapeDtypeStruct((modes, rows) + lateral, jnp.float32),
            jax.ShapeDtypeStruct(decay.shape, jnp.float32),
            jax.ShapeDtypeStruct(decay.shape, jnp.float32),
            jax.ShapeDtypeStruct((copies, 2 + 2 * modes) + lateral, jnp.float32),
        ),
    )(mixed, decay)


def local(fields, mean_field, kl_modes, decay, coupling, pattern, mode_order):
    local_modes = fields.shape[0]
    rows = fields.shape[1]
    lateral = fields.shape[2:]
    mode_total = mode_order.shape[0]
    groups = lax.axis_size("mode")
    chunk = rows // groups
    masked = coupling * pattern.astype(jnp.float32)
    coupling_table = jnp.take(jnp.take(masked, mode_order, axis=0), mode_order, axis=1)
    term_total = coupling_table.shape[2]

    slabs = lax.axis_size("depth")
    from_below = lax.ppermute(fields[:, -1], "depth", [(i, i + 1) for i in range(slabs - 1)])
    from_above = lax.ppermute(fields[:, 0], "depth", [(i + 1, i) for i in range(slabs - 1)])
    stencil = slab_stencil(fields, from_below, from_above)
    stencil = jnp.transpose(stencil, (1, 0, 2, 3))
    stencil_rows = lax.all_to_all(stencil, "mode", 1, 0, tiled=True)
    cell_count = chunk * lateral[0] * lateral[1]
    stencil_rows = stencil_rows.reshape(mode_total, cell_count)

    coefficients = jnp.concatenate([mean_field[None], kl_modes], axis=0)
    my_chunk = lax.axis_index("mode") * chunk
    coefficients = lax.dynamic_slice_in_dim(coefficients, my_chunk, chunk, axis=1)
    coefficients = coefficients.reshape(term_total, 1, cell_count)

    table_rows = jnp.transpose(coupling_table, (2, 0, 1)).reshape(term_total * mode_total, mode_total)
    accumulated = jnp.dot(
        table_rows,
        stencil_rows,
        precision=lax.Precision.HIGH,
        preferred_element_type=jnp.float32,
    ).reshape(term_total, mode_total, cell_count)
    mixed_rows = jnp.sum(coefficients * accumulated, axis=0)
    mixed_rows = mixed_rows.reshape((mode_total, chunk) + lateral)
    mixed_field = lax.all_to_all(mixed_rows, "mode", 0, 0, tiled=True)
    mixed_field = mixed_field.reshape((groups, local_modes, chunk) + lateral)

    back, coupled, tail, copies = local_sweeps(mixed_field, decay, slabs)
    summaries = lax.all_to_all(copies, "depth", 0, 0, tiled=True)
    ratio_all = summaries[:, 0]
    coupled_all = summaries[:, 1]
    forward_all = summaries[:, 2 : 2 + local_modes]
    back_all = summaries[:, 2 + local_modes :]

    me = lax.axis_index("depth")
    entering = [jnp.zeros_like(forward_all[0])]
    for slab in range(slabs - 1):
        entering.append(ratio_all[slab][None] * entering[-1] + forward_all[slab])
    low = entering[0]
    for slab in range(1, slabs):
        low = jnp.where(me == slab, entering[slab], low)
    above = jnp.zeros_like(forward_all[0])
    high = above
    for slab in range(slabs - 1, 0, -1):
        above = (
            back_all[slab]
            + coupled_all[slab][None] * entering[slab]
            + ratio_all[slab][None] * above
        )
        high = jnp.where(me == slab - 1, above, high)
    return back + coupled[None] * low[:, None] + tail[None] * high[:, None]


def solution(mesh):
    in_specs = (
        P("mode", "depth", None, None),
        P("depth", None, None),
        P(None, "depth", None, None),
        P("depth", None, None),
        P(),
        P(),
        P(),
    )
    out_specs = P("mode", "depth", None, None)
    return jax.shard_map(local, mesh=mesh, in_specs=in_specs, out_specs=out_specs, check_vma=False)
```

```python
import jax
import jax.numpy as jnp
from jax import lax
from jax.experimental import pallas as pl
from jax.experimental.pallas import tpu as pltpu
from jax.sharding import PartitionSpec as P


def neighbour_masks(shape, axis):
    size = shape[axis]
    where_from = lax.broadcasted_iota(jnp.int32, shape, axis)
    return [
        (shift, jnp.abs(pltpu.roll(where_from, shift, axis) - where_from) == 1)
        for shift in (1, size - 1)
    ]


def stencil_kernel(fields_ref, out_ref):
    rows = fields_ref.shape[1]
    plane = fields_ref.shape[2:]
    masks = neighbour_masks(plane, 0) + neighbour_masks(plane, 1)
    axes = [0, 0, 1, 1]
    for z in range(rows):
        centre = fields_ref[0, z]
        beside = jnp.zeros_like(centre)
        if z + 1 < rows:
            beside = beside + fields_ref[0, z + 1]
        if z > 0:
            beside = beside + fields_ref[0, z - 1]
        for axis, (shift, inside) in zip(axes, masks):
            beside = beside + jnp.where(inside, pltpu.roll(centre, shift, axis), 0.0)
        out_ref[z, 0] = 6.0 * centre - beside


def slab_stencil(fields):
    modes, rows = fields.shape[0], fields.shape[1]
    plane = fields.shape[2:]
    return pl.pallas_call(
        stencil_kernel,
        grid=(modes,),
        in_specs=[pl.BlockSpec((1, rows) + plane, lambda i: (i, 0, 0, 0))],
        out_specs=pl.BlockSpec((rows, 1) + plane, lambda i: (0, i, 0, 0)),
        out_shape=jax.ShapeDtypeStruct((rows, modes) + plane, jnp.float32),
    )(fields)


def edge_kernel(stencil_ref, below_ref, above_ref, out_ref):
    halo = jnp.where(pl.program_id(0) == 0, below_ref[...], above_ref[...])
    out_ref[...] = stencil_ref[...] - halo[None]


def add_edges(stencil, below, above):
    rows = stencil.shape[0]
    edge = (1,) + stencil.shape[1:]
    at_edge = lambda i: (i * (rows - 1), 0, 0, 0)
    return pl.pallas_call(
        edge_kernel,
        grid=(2,),
        in_specs=[
            pl.BlockSpec(edge, at_edge),
            pl.BlockSpec(below.shape, lambda i: (0, 0, 0)),
            pl.BlockSpec(above.shape, lambda i: (0, 0, 0)),
        ],
        out_specs=pl.BlockSpec(edge, at_edge),
        out_shape=jax.ShapeDtypeStruct(stencil.shape, jnp.float32),
        input_output_aliases={0: 0},
    )(stencil, below, above)


def sweep_kernel(mixed_ref, decay_ref, back_ref, coupled_ref, tail_ref, summary_ref):
    rows = decay_ref.shape[0]
    chunk = mixed_ref.shape[2]

    def forward_row(z, carried):
        state, ratio = carried
        d = decay_ref[z]
        g = jnp.sqrt(1.0 - d * d)
        state = d[None] * state + g[None] * mixed_ref[z // chunk, :, z % chunk]
        ratio = d * ratio
        back_ref[:, z] = g[None] * state
        coupled_ref[z] = g * ratio
        return state, ratio

    lateral = decay_ref.shape[1:]
    modes = mixed_ref.shape[1]
    state, _ = lax.fori_loop(
        0,
        rows,
        forward_row,
        (jnp.zeros((modes,) + lateral, jnp.float32), jnp.ones(lateral, jnp.float32)),
    )

    def backward_row(i, carried):
        z = rows - 1 - i
        back, coupled, tail = carried
        d = decay_ref[z]
        back = d[None] * back + back_ref[:, z]
        coupled = d * coupled + coupled_ref[z]
        tail = d * tail
        back_ref[:, z] = back
        coupled_ref[z] = coupled
        tail_ref[z] = tail
        return back, coupled, tail

    back, coupled, tail = lax.fori_loop(
        0,
        rows,
        backward_row,
        (
            jnp.zeros((modes,) + lateral, jnp.float32),
            jnp.zeros(lateral, jnp.float32),
            jnp.ones(lateral, jnp.float32),
        ),
    )
    for copy in range(summary_ref.shape[0]):
        summary_ref[copy, 0] = tail
        summary_ref[copy, 1] = coupled
        summary_ref[copy, 2 : 2 + modes] = state
        summary_ref[copy, 2 + modes :] = back


def local_sweeps(mixed, decay, copies):
    modes = mixed.shape[1]
    rows = decay.shape[0]
    lateral = decay.shape[1:]
    return pl.pallas_call(
        sweep_kernel,
        out_shape=(
            jax.ShapeDtypeStruct((modes, rows) + lateral, jnp.float32),
            jax.ShapeDtypeStruct(decay.shape, jnp.float32),
            jax.ShapeDtypeStruct(decay.shape, jnp.float32),
            jax.ShapeDtypeStruct((copies, 2 + 2 * modes) + lateral, jnp.float32),
        ),
    )(mixed, decay)


def local(fields, mean_field, kl_modes, decay, coupling, pattern, mode_order):
    local_modes = fields.shape[0]
    rows = fields.shape[1]
    lateral = fields.shape[2:]
    mode_total = mode_order.shape[0]
    groups = lax.axis_size("mode")
    chunk = rows // groups
    masked = coupling * pattern.astype(jnp.float32)
    coupling_table = jnp.take(jnp.take(masked, mode_order, axis=0), mode_order, axis=1)
    term_total = coupling_table.shape[2]

    slabs = lax.axis_size("depth")
    from_below = lax.ppermute(fields[:, -1], "depth", [(i, i + 1) for i in range(slabs - 1)])
    from_above = lax.ppermute(fields[:, 0], "depth", [(i + 1, i) for i in range(slabs - 1)])
    stencil = add_edges(slab_stencil(fields), from_below, from_above)
    stencil = jnp.transpose(stencil, (1, 0, 2, 3))
    stencil_rows = lax.all_to_all(stencil, "mode", 1, 0, tiled=True)
    cell_count = chunk * lateral[0] * lateral[1]
    stencil_rows = stencil_rows.reshape(mode_total, cell_count)

    coefficients = jnp.concatenate([mean_field[None], kl_modes], axis=0)
    my_chunk = lax.axis_index("mode") * chunk
    coefficients = lax.dynamic_slice_in_dim(coefficients, my_chunk, chunk, axis=1)
    coefficients = coefficients.reshape(term_total, 1, cell_count)

    table_rows = jnp.transpose(coupling_table, (2, 0, 1)).reshape(term_total * mode_total, mode_total)
    accumulated = jnp.dot(
        table_rows,
        stencil_rows,
        precision=lax.Precision.HIGH,
        preferred_element_type=jnp.float32,
    ).reshape(term_total, mode_total, cell_count)
    mixed_rows = jnp.sum(coefficients * accumulated, axis=0)
    mixed_rows = mixed_rows.reshape((mode_total, chunk) + lateral)
    mixed_field = lax.all_to_all(mixed_rows, "mode", 0, 0, tiled=True)
    mixed_field = mixed_field.reshape((groups, local_modes, chunk) + lateral)

    back, coupled, tail, copies = local_sweeps(mixed_field, decay, slabs)
    summaries = lax.all_to_all(copies, "depth", 0, 0, tiled=True)
    ratio_all = summaries[:, 0]
    coupled_all = summaries[:, 1]
    forward_all = summaries[:, 2 : 2 + local_modes]
    back_all = summaries[:, 2 + local_modes :]

    me = lax.axis_index("depth")
    entering = [jnp.zeros_like(forward_all[0])]
    for slab in range(slabs - 1):
        entering.append(ratio_all[slab][None] * entering[-1] + forward_all[slab])
    low = entering[0]
    for slab in range(1, slabs):
        low = jnp.where(me == slab, entering[slab], low)
    above = jnp.zeros_like(forward_all[0])
    high = above
    for slab in range(slabs - 1, 0, -1):
        above = (
            back_all[slab]
            + coupled_all[slab][None] * entering[slab]
            + ratio_all[slab][None] * above
        )
        high = jnp.where(me == slab - 1, above, high)
    return back + coupled[None] * low[:, None] + tail[None] * high[:, None]


def solution(mesh):
    in_specs = (
        P("mode", "depth", None, None),
        P("depth", None, None),
        P(None, "depth", None, None),
        P("depth", None, None),
        P(),
        P(),
        P(),
    )
    out_specs = P("mode", "depth", None, None)
    return jax.shard_map(local, mesh=mesh, in_specs=in_specs, out_specs=out_specs, check_vma=False)
```

```python
import jax
import jax.numpy as jnp
from jax import lax
from jax.experimental import pallas as pl
from jax.experimental.pallas import tpu as pltpu
from jax.sharding import PartitionSpec as P


def neighbour_masks(shape, axis):
    size = shape[axis]
    where_from = lax.broadcasted_iota(jnp.int32, shape, axis)
    return [
        (shift, jnp.abs(pltpu.roll(where_from, shift, axis) - where_from) == 1)
        for shift in (1, size - 1)
    ]


def stencil_kernel(fields_ref, out_ref):
    rows = fields_ref.shape[1]
    plane = fields_ref.shape[2:]
    masks = neighbour_masks(plane, 0) + neighbour_masks(plane, 1)
    axes = [0, 0, 1, 1]
    for z in range(rows):
        centre = fields_ref[0, z]
        beside = jnp.zeros_like(centre)
        if z + 1 < rows:
            beside = beside + fields_ref[0, z + 1]
        if z > 0:
            beside = beside + fields_ref[0, z - 1]
        for axis, (shift, inside) in zip(axes, masks):
            beside = beside + jnp.where(inside, pltpu.roll(centre, shift, axis), 0.0)
        out_ref[z, 0] = 6.0 * centre - beside


def slab_stencil(fields):
    modes, rows = fields.shape[0], fields.shape[1]
    plane = fields.shape[2:]
    return pl.pallas_call(
        stencil_kernel,
        grid=(modes,),
        in_specs=[pl.BlockSpec((1, rows) + plane, lambda i: (i, 0, 0, 0))],
        out_specs=pl.BlockSpec((rows, 1) + plane, lambda i: (0, i, 0, 0)),
        out_shape=jax.ShapeDtypeStruct((rows, modes) + plane, jnp.float32),
    )(fields)


def edge_kernel(stencil_ref, below_ref, above_ref, out_ref):
    halo = jnp.where(pl.program_id(0) == 0, below_ref[...], above_ref[...])
    out_ref[...] = stencil_ref[...] - halo[None]


def add_edges(stencil, below, above):
    rows = stencil.shape[0]
    edge = (1,) + stencil.shape[1:]
    at_edge = lambda i: (i * (rows - 1), 0, 0, 0)
    return pl.pallas_call(
        edge_kernel,
        grid=(2,),
        in_specs=[
            pl.BlockSpec(edge, at_edge),
            pl.BlockSpec(below.shape, lambda i: (0, 0, 0)),
            pl.BlockSpec(above.shape, lambda i: (0, 0, 0)),
        ],
        out_specs=pl.BlockSpec(edge, at_edge),
        out_shape=jax.ShapeDtypeStruct(stencil.shape, jnp.float32),
        input_output_aliases={0: 0},
    )(stencil, below, above)


def sweep_kernel(mixed_ref, decay_ref, back_ref, coupled_ref, tail_ref, summary_ref):
    rows = decay_ref.shape[0]
    chunk = mixed_ref.shape[2]

    def forward_row(z, carried):
        state, ratio = carried
        d = decay_ref[z]
        g = jnp.sqrt(1.0 - d * d)
        state = d[None] * state + g[None] * mixed_ref[z // chunk, :, z % chunk]
        ratio = d * ratio
        back_ref[:, z] = g[None] * state
        coupled_ref[z] = g * ratio
        return state, ratio

    lateral = decay_ref.shape[1:]
    modes = mixed_ref.shape[1]
    state, _ = lax.fori_loop(
        0,
        rows,
        forward_row,
        (jnp.zeros((modes,) + lateral, jnp.float32), jnp.ones(lateral, jnp.float32)),
    )

    def backward_row(i, carried):
        z = rows - 1 - i
        back, coupled, tail = carried
        d = decay_ref[z]
        back = d[None] * back + back_ref[:, z]
        coupled = d * coupled + coupled_ref[z]
        tail = d * tail
        back_ref[:, z] = back
        coupled_ref[z] = coupled
        tail_ref[z] = tail
        return back, coupled, tail

    back, coupled, tail = lax.fori_loop(
        0,
        rows,
        backward_row,
        (
            jnp.zeros((modes,) + lateral, jnp.float32),
            jnp.zeros(lateral, jnp.float32),
            jnp.ones(lateral, jnp.float32),
        ),
    )
    for copy in range(summary_ref.shape[0]):
        summary_ref[copy, 0] = tail
        summary_ref[copy, 1] = coupled
        summary_ref[copy, 2 : 2 + modes] = state
        summary_ref[copy, 2 + modes :] = back


def local_sweeps(mixed, decay, copies):
    groups, modes, chunk = mixed.shape[0], mixed.shape[1], mixed.shape[2]
    rows = decay.shape[0]
    lateral = decay.shape[1:]
    parts = 2
    half = (lateral[0] // parts, lateral[1])
    return pl.pallas_call(
        sweep_kernel,
        grid=(parts,),
        in_specs=[
            pl.BlockSpec((groups, modes, chunk) + half, lambda i: (0, 0, 0, i, 0)),
            pl.BlockSpec((rows,) + half, lambda i: (0, i, 0)),
        ],
        out_specs=(
            pl.BlockSpec((modes, rows) + half, lambda i: (0, 0, i, 0)),
            pl.BlockSpec((rows,) + half, lambda i: (0, i, 0)),
            pl.BlockSpec((rows,) + half, lambda i: (0, i, 0)),
            pl.BlockSpec((copies, 2 + 2 * modes) + half, lambda i: (0, 0, i, 0)),
        ),
        out_shape=(
            jax.ShapeDtypeStruct((modes, rows) + lateral, jnp.float32),
            jax.ShapeDtypeStruct(decay.shape, jnp.float32),
            jax.ShapeDtypeStruct(decay.shape, jnp.float32),
            jax.ShapeDtypeStruct((copies, 2 + 2 * modes) + lateral, jnp.float32),
        ),
    )(mixed, decay)


def local(fields, mean_field, kl_modes, decay, coupling, pattern, mode_order):
    local_modes = fields.shape[0]
    rows = fields.shape[1]
    lateral = fields.shape[2:]
    mode_total = mode_order.shape[0]
    groups = lax.axis_size("mode")
    chunk = rows // groups
    masked = coupling * pattern.astype(jnp.float32)
    coupling_table = jnp.take(jnp.take(masked, mode_order, axis=0), mode_order, axis=1)
    term_total = coupling_table.shape[2]

    slabs = lax.axis_size("depth")
    from_below = lax.ppermute(fields[:, -1], "depth", [(i, i + 1) for i in range(slabs - 1)])
    from_above = lax.ppermute(fields[:, 0], "depth", [(i + 1, i) for i in range(slabs - 1)])
    stencil = add_edges(slab_stencil(fields), from_below, from_above)
    stencil = jnp.transpose(stencil, (1, 0, 2, 3))
    stencil_rows = lax.all_to_all(stencil, "mode", 1, 0, tiled=True)
    cell_count = chunk * lateral[0] * lateral[1]
    stencil_rows = stencil_rows.reshape(mode_total, cell_count)

    coefficients = jnp.concatenate([mean_field[None], kl_modes], axis=0)
    my_chunk = lax.axis_index("mode") * chunk
    coefficients = lax.dynamic_slice_in_dim(coefficients, my_chunk, chunk, axis=1)
    coefficients = coefficients.reshape(term_total, 1, cell_count)

    table_rows = jnp.transpose(coupling_table, (2, 0, 1)).reshape(term_total * mode_total, mode_total)
    accumulated = jnp.dot(
        table_rows,
        stencil_rows,
        precision=lax.Precision.HIGH,
        preferred_element_type=jnp.float32,
    ).reshape(term_total, mode_total, cell_count)
    mixed_rows = jnp.sum(coefficients * accumulated, axis=0)
    mixed_rows = mixed_rows.reshape((mode_total, chunk) + lateral)
    mixed_field = lax.all_to_all(mixed_rows, "mode", 0, 0, tiled=True)
    mixed_field = mixed_field.reshape((groups, local_modes, chunk) + lateral)

    back, coupled, tail, copies = local_sweeps(mixed_field, decay, slabs)
    summaries = lax.all_to_all(copies, "depth", 0, 0, tiled=True)
    ratio_all = summaries[:, 0]
    coupled_all = summaries[:, 1]
    forward_all = summaries[:, 2 : 2 + local_modes]
    back_all = summaries[:, 2 + local_modes :]

    me = lax.axis_index("depth")
    entering = [jnp.zeros_like(forward_all[0])]
    for slab in range(slabs - 1):
        entering.append(ratio_all[slab][None] * entering[-1] + forward_all[slab])
    low = entering[0]
    for slab in range(1, slabs):
        low = jnp.where(me == slab, entering[slab], low)
    above = jnp.zeros_like(forward_all[0])
    high = above
    for slab in range(slabs - 1, 0, -1):
        above = (
            back_all[slab]
            + coupled_all[slab][None] * entering[slab]
            + ratio_all[slab][None] * above
        )
        high = jnp.where(me == slab - 1, above, high)
    return back + coupled[None] * low[:, None] + tail[None] * high[:, None]


def solution(mesh):
    in_specs = (
        P("mode", "depth", None, None),
        P("depth", None, None),
        P(None, "depth", None, None),
        P("depth", None, None),
        P(),
        P(),
        P(),
    )
    out_specs = P("mode", "depth", None, None)
    return jax.shard_map(local, mesh=mesh, in_specs=in_specs, out_specs=out_specs, check_vma=False)
```

```python
import jax
import jax.numpy as jnp
from jax import lax
from jax.experimental import pallas as pl
from jax.experimental.pallas import tpu as pltpu
from jax.sharding import PartitionSpec as P


def neighbour_masks(shape, axis):
    size = shape[axis]
    where_from = lax.broadcasted_iota(jnp.int32, shape, axis)
    return [
        (shift, jnp.abs(pltpu.roll(where_from, shift, axis) - where_from) == 1)
        for shift in (1, size - 1)
    ]


def stencil_kernel(fields_ref, out_ref):
    rows = fields_ref.shape[1]
    plane = fields_ref.shape[2:]
    masks = neighbour_masks(plane, 0) + neighbour_masks(plane, 1)
    axes = [0, 0, 1, 1]
    for z in range(rows):
        centre = fields_ref[0, z]
        beside = jnp.zeros_like(centre)
        if z + 1 < rows:
            beside = beside + fields_ref[0, z + 1]
        if z > 0:
            beside = beside + fields_ref[0, z - 1]
        for axis, (shift, inside) in zip(axes, masks):
            beside = beside + jnp.where(inside, pltpu.roll(centre, shift, axis), 0.0)
        out_ref[z, 0] = 6.0 * centre - beside


def slab_stencil(fields):
    modes, rows = fields.shape[0], fields.shape[1]
    plane = fields.shape[2:]
    return pl.pallas_call(
        stencil_kernel,
        grid=(modes,),
        in_specs=[pl.BlockSpec((1, rows) + plane, lambda i: (i, 0, 0, 0))],
        out_specs=pl.BlockSpec((rows, 1) + plane, lambda i: (0, i, 0, 0)),
        out_shape=jax.ShapeDtypeStruct((rows, modes) + plane, jnp.float32),
    )(fields)


def edge_kernel(stencil_ref, below_ref, above_ref, out_ref):
    halo = jnp.where(pl.program_id(0) == 0, below_ref[...], above_ref[...])
    out_ref[...] = stencil_ref[...] - halo[None]


def add_edges(stencil, below, above):
    rows = stencil.shape[0]
    edge = (1,) + stencil.shape[1:]
    at_edge = lambda i: (i * (rows - 1), 0, 0, 0)
    return pl.pallas_call(
        edge_kernel,
        grid=(2,),
        in_specs=[
            pl.BlockSpec(edge, at_edge),
            pl.BlockSpec(below.shape, lambda i: (0, 0, 0)),
            pl.BlockSpec(above.shape, lambda i: (0, 0, 0)),
        ],
        out_specs=pl.BlockSpec(edge, at_edge),
        out_shape=jax.ShapeDtypeStruct(stencil.shape, jnp.float32),
        input_output_aliases={0: 0},
    )(stencil, below, above)


def sweep_kernel(mixed_ref, decay_ref, back_ref, coupled_ref, tail_ref, summary_ref):
    rows = decay_ref.shape[0]
    chunk = mixed_ref.shape[2]

    def forward_row(z, carried):
        state, ratio = carried
        d = decay_ref[z]
        g = jnp.sqrt(1.0 - d * d)
        state = d[None] * state + g[None] * mixed_ref[z // chunk, :, z % chunk]
        ratio = d * ratio
        back_ref[:, z] = g[None] * state
        coupled_ref[z] = g * ratio
        return state, ratio

    lateral = decay_ref.shape[1:]
    modes = mixed_ref.shape[1]
    state, _ = lax.fori_loop(
        0,
        rows,
        forward_row,
        (jnp.zeros((modes,) + lateral, jnp.float32), jnp.ones(lateral, jnp.float32)),
        unroll=True,
    )

    def backward_row(i, carried):
        z = rows - 1 - i
        back, coupled, tail = carried
        d = decay_ref[z]
        back = d[None] * back + back_ref[:, z]
        coupled = d * coupled + coupled_ref[z]
        tail = d * tail
        back_ref[:, z] = back
        coupled_ref[z] = coupled
        tail_ref[z] = tail
        return back, coupled, tail

    back, coupled, tail = lax.fori_loop(
        0,
        rows,
        backward_row,
        (
            jnp.zeros((modes,) + lateral, jnp.float32),
            jnp.zeros(lateral, jnp.float32),
            jnp.ones(lateral, jnp.float32),
        ),
        unroll=True,
    )
    for copy in range(summary_ref.shape[0]):
        summary_ref[copy, 0] = tail
        summary_ref[copy, 1] = coupled
        summary_ref[copy, 2 : 2 + modes] = state
        summary_ref[copy, 2 + modes :] = back


def local_sweeps(mixed, decay, copies):
    groups, modes, chunk = mixed.shape[0], mixed.shape[1], mixed.shape[2]
    rows = decay.shape[0]
    lateral = decay.shape[1:]
    parts = 2
    half = (lateral[0] // parts, lateral[1])
    return pl.pallas_call(
        sweep_kernel,
        grid=(parts,),
        in_specs=[
            pl.BlockSpec((groups, modes, chunk) + half, lambda i: (0, 0, 0, i, 0)),
            pl.BlockSpec((rows,) + half, lambda i: (0, i, 0)),
        ],
        out_specs=(
            pl.BlockSpec((modes, rows) + half, lambda i: (0, 0, i, 0)),
            pl.BlockSpec((rows,) + half, lambda i: (0, i, 0)),
            pl.BlockSpec((rows,) + half, lambda i: (0, i, 0)),
            pl.BlockSpec((copies, 2 + 2 * modes) + half, lambda i: (0, 0, i, 0)),
        ),
        out_shape=(
            jax.ShapeDtypeStruct((modes, rows) + lateral, jnp.float32),
            jax.ShapeDtypeStruct(decay.shape, jnp.float32),
            jax.ShapeDtypeStruct(decay.shape, jnp.float32),
            jax.ShapeDtypeStruct((copies, 2 + 2 * modes) + lateral, jnp.float32),
        ),
    )(mixed, decay)


def local(fields, mean_field, kl_modes, decay, coupling, pattern, mode_order):
    local_modes = fields.shape[0]
    rows = fields.shape[1]
    lateral = fields.shape[2:]
    mode_total = mode_order.shape[0]
    groups = lax.axis_size("mode")
    chunk = rows // groups
    masked = coupling * pattern.astype(jnp.float32)
    coupling_table = jnp.take(jnp.take(masked, mode_order, axis=0), mode_order, axis=1)
    term_total = coupling_table.shape[2]

    slabs = lax.axis_size("depth")
    from_below = lax.ppermute(fields[:, -1], "depth", [(i, i + 1) for i in range(slabs - 1)])
    from_above = lax.ppermute(fields[:, 0], "depth", [(i + 1, i) for i in range(slabs - 1)])
    stencil = add_edges(slab_stencil(fields), from_below, from_above)
    stencil = jnp.transpose(stencil, (1, 0, 2, 3))
    stencil_rows = lax.all_to_all(stencil, "mode", 1, 0, tiled=True)
    cell_count = chunk * lateral[0] * lateral[1]
    stencil_rows = stencil_rows.reshape(mode_total, cell_count)

    coefficients = jnp.concatenate([mean_field[None], kl_modes], axis=0)
    my_chunk = lax.axis_index("mode") * chunk
    coefficients = lax.dynamic_slice_in_dim(coefficients, my_chunk, chunk, axis=1)
    coefficients = coefficients.reshape(term_total, 1, cell_count)

    table_rows = jnp.transpose(coupling_table, (2, 0, 1)).reshape(term_total * mode_total, mode_total)
    accumulated = jnp.dot(
        table_rows,
        stencil_rows,
        precision=lax.Precision.HIGH,
        preferred_element_type=jnp.float32,
    ).reshape(term_total, mode_total, cell_count)
    mixed_rows = jnp.sum(coefficients * accumulated, axis=0)
    mixed_rows = mixed_rows.reshape((mode_total, chunk) + lateral)
    mixed_field = lax.all_to_all(mixed_rows, "mode", 0, 0, tiled=True)
    mixed_field = mixed_field.reshape((groups, local_modes, chunk) + lateral)

    back, coupled, tail, copies = local_sweeps(mixed_field, decay, slabs)
    summaries = lax.all_to_all(copies, "depth", 0, 0, tiled=True)
    ratio_all = summaries[:, 0]
    coupled_all = summaries[:, 1]
    forward_all = summaries[:, 2 : 2 + local_modes]
    back_all = summaries[:, 2 + local_modes :]

    me = lax.axis_index("depth")
    entering = [jnp.zeros_like(forward_all[0])]
    for slab in range(slabs - 1):
        entering.append(ratio_all[slab][None] * entering[-1] + forward_all[slab])
    low = entering[0]
    for slab in range(1, slabs):
        low = jnp.where(me == slab, entering[slab], low)
    above = jnp.zeros_like(forward_all[0])
    high = above
    for slab in range(slabs - 1, 0, -1):
        above = (
            back_all[slab]
            + coupled_all[slab][None] * entering[slab]
            + ratio_all[slab][None] * above
        )
        high = jnp.where(me == slab - 1, above, high)
    return back + coupled[None] * low[:, None] + tail[None] * high[:, None]


def solution(mesh):
    in_specs = (
        P("mode", "depth", None, None),
        P("depth", None, None),
        P(None, "depth", None, None),
        P("depth", None, None),
        P(),
        P(),
        P(),
    )
    out_specs = P("mode", "depth", None, None)
    return jax.shard_map(local, mesh=mesh, in_specs=in_specs, out_specs=out_specs, check_vma=False)
```

```python
import jax
import jax.numpy as jnp
from jax import lax
from jax.experimental import pallas as pl
from jax.experimental.pallas import tpu as pltpu
from jax.sharding import PartitionSpec as P


def neighbour_masks(shape, axis):
    size = shape[axis]
    where_from = lax.broadcasted_iota(jnp.int32, shape, axis)
    return [
        (shift, jnp.abs(pltpu.roll(where_from, shift, axis) - where_from) == 1)
        for shift in (1, size - 1)
    ]


def stencil_kernel(fields_ref, out_ref):
    modes, rows = fields_ref.shape[0], fields_ref.shape[1]
    plane = fields_ref.shape[2:]
    masks = neighbour_masks(plane, 0) + neighbour_masks(plane, 1)
    axes = [0, 0, 1, 1]
    for mode in range(modes):
        for z in range(rows):
            centre = fields_ref[mode, z]
            beside = jnp.zeros_like(centre)
            if z + 1 < rows:
                beside = beside + fields_ref[mode, z + 1]
            if z > 0:
                beside = beside + fields_ref[mode, z - 1]
            for axis, (shift, inside) in zip(axes, masks):
                beside = beside + jnp.where(inside, pltpu.roll(centre, shift, axis), 0.0)
            out_ref[z, mode] = 6.0 * centre - beside


def slab_stencil(fields):
    modes, rows = fields.shape[0], fields.shape[1]
    plane = fields.shape[2:]
    return pl.pallas_call(
        stencil_kernel,
        out_shape=jax.ShapeDtypeStruct((rows, modes) + plane, jnp.float32),
    )(fields)


def edge_kernel(stencil_ref, below_ref, above_ref, out_ref):
    halo = jnp.where(pl.program_id(0) == 0, below_ref[...], above_ref[...])
    out_ref[...] = stencil_ref[...] - halo[None]


def add_edges(stencil, below, above):
    rows = stencil.shape[0]
    edge = (1,) + stencil.shape[1:]
    at_edge = lambda i: (i * (rows - 1), 0, 0, 0)
    return pl.pallas_call(
        edge_kernel,
        grid=(2,),
        in_specs=[
            pl.BlockSpec(edge, at_edge),
            pl.BlockSpec(below.shape, lambda i: (0, 0, 0)),
            pl.BlockSpec(above.shape, lambda i: (0, 0, 0)),
        ],
        out_specs=pl.BlockSpec(edge, at_edge),
        out_shape=jax.ShapeDtypeStruct(stencil.shape, jnp.float32),
        input_output_aliases={0: 0},
    )(stencil, below, above)


def sweep_kernel(mixed_ref, decay_ref, back_ref, coupled_ref, tail_ref, summary_ref):
    rows = decay_ref.shape[0]
    chunk = mixed_ref.shape[2]

    def forward_row(z, carried):
        state, ratio = carried
        d = decay_ref[z]
        g = jnp.sqrt(1.0 - d * d)
        state = d[None] * state + g[None] * mixed_ref[z // chunk, :, z % chunk]
        ratio = d * ratio
        back_ref[:, z] = g[None] * state
        coupled_ref[z] = g * ratio
        return state, ratio

    lateral = decay_ref.shape[1:]
    modes = mixed_ref.shape[1]
    state, _ = lax.fori_loop(
        0,
        rows,
        forward_row,
        (jnp.zeros((modes,) + lateral, jnp.float32), jnp.ones(lateral, jnp.float32)),
        unroll=True,
    )

    def backward_row(i, carried):
        z = rows - 1 - i
        back, coupled, tail = carried
        d = decay_ref[z]
        back = d[None] * back + back_ref[:, z]
        coupled = d * coupled + coupled_ref[z]
        tail = d * tail
        back_ref[:, z] = back
        coupled_ref[z] = coupled
        tail_ref[z] = tail
        return back, coupled, tail

    back, coupled, tail = lax.fori_loop(
        0,
        rows,
        backward_row,
        (
            jnp.zeros((modes,) + lateral, jnp.float32),
            jnp.zeros(lateral, jnp.float32),
            jnp.ones(lateral, jnp.float32),
        ),
        unroll=True,
    )
    for copy in range(summary_ref.shape[0]):
        summary_ref[copy, 0] = tail
        summary_ref[copy, 1] = coupled
        summary_ref[copy, 2 : 2 + modes] = state
        summary_ref[copy, 2 + modes :] = back


def local_sweeps(mixed, decay, copies):
    groups, modes, chunk = mixed.shape[0], mixed.shape[1], mixed.shape[2]
    rows = decay.shape[0]
    lateral = decay.shape[1:]
    parts = 2
    half = (lateral[0] // parts, lateral[1])
    return pl.pallas_call(
        sweep_kernel,
        grid=(parts,),
        in_specs=[
            pl.BlockSpec((groups, modes, chunk) + half, lambda i: (0, 0, 0, i, 0)),
            pl.BlockSpec((rows,) + half, lambda i: (0, i, 0)),
        ],
        out_specs=(
            pl.BlockSpec((modes, rows) + half, lambda i: (0, 0, i, 0)),
            pl.BlockSpec((rows,) + half, lambda i: (0, i, 0)),
            pl.BlockSpec((rows,) + half, lambda i: (0, i, 0)),
            pl.BlockSpec((copies, 2 + 2 * modes) + half, lambda i: (0, 0, i, 0)),
        ),
        out_shape=(
            jax.ShapeDtypeStruct((modes, rows) + lateral, jnp.float32),
            jax.ShapeDtypeStruct(decay.shape, jnp.float32),
            jax.ShapeDtypeStruct(decay.shape, jnp.float32),
            jax.ShapeDtypeStruct((copies, 2 + 2 * modes) + lateral, jnp.float32),
        ),
    )(mixed, decay)


def local(fields, mean_field, kl_modes, decay, coupling, pattern, mode_order):
    local_modes = fields.shape[0]
    rows = fields.shape[1]
    lateral = fields.shape[2:]
    mode_total = mode_order.shape[0]
    groups = lax.axis_size("mode")
    chunk = rows // groups
    masked = coupling * pattern.astype(jnp.float32)
    coupling_table = jnp.take(jnp.take(masked, mode_order, axis=0), mode_order, axis=1)
    term_total = coupling_table.shape[2]

    slabs = lax.axis_size("depth")
    from_below = lax.ppermute(fields[:, -1], "depth", [(i, i + 1) for i in range(slabs - 1)])
    from_above = lax.ppermute(fields[:, 0], "depth", [(i + 1, i) for i in range(slabs - 1)])
    stencil = add_edges(slab_stencil(fields), from_below, from_above)
    stencil = jnp.transpose(stencil, (1, 0, 2, 3))
    stencil_rows = lax.all_to_all(stencil, "mode", 1, 0, tiled=True)
    cell_count = chunk * lateral[0] * lateral[1]
    stencil_rows = stencil_rows.reshape(mode_total, cell_count)

    coefficients = jnp.concatenate([mean_field[None], kl_modes], axis=0)
    my_chunk = lax.axis_index("mode") * chunk
    coefficients = lax.dynamic_slice_in_dim(coefficients, my_chunk, chunk, axis=1)
    coefficients = coefficients.reshape(term_total, 1, cell_count)

    table_rows = jnp.transpose(coupling_table, (2, 0, 1)).reshape(term_total * mode_total, mode_total)
    accumulated = jnp.dot(
        table_rows,
        stencil_rows,
        precision=lax.Precision.HIGH,
        preferred_element_type=jnp.float32,
    ).reshape(term_total, mode_total, cell_count)
    mixed_rows = jnp.sum(coefficients * accumulated, axis=0)
    mixed_rows = mixed_rows.reshape((mode_total, chunk) + lateral)
    mixed_field = lax.all_to_all(mixed_rows, "mode", 0, 0, tiled=True)
    mixed_field = mixed_field.reshape((groups, local_modes, chunk) + lateral)

    back, coupled, tail, copies = local_sweeps(mixed_field, decay, slabs)
    summaries = lax.all_to_all(copies, "depth", 0, 0, tiled=True)
    ratio_all = summaries[:, 0]
    coupled_all = summaries[:, 1]
    forward_all = summaries[:, 2 : 2 + local_modes]
    back_all = summaries[:, 2 + local_modes :]

    me = lax.axis_index("depth")
    entering = [jnp.zeros_like(forward_all[0])]
    for slab in range(slabs - 1):
        entering.append(ratio_all[slab][None] * entering[-1] + forward_all[slab])
    low = entering[0]
    for slab in range(1, slabs):
        low = jnp.where(me == slab, entering[slab], low)
    above = jnp.zeros_like(forward_all[0])
    high = above
    for slab in range(slabs - 1, 0, -1):
        above = (
            back_all[slab]
            + coupled_all[slab][None] * entering[slab]
            + ratio_all[slab][None] * above
        )
        high = jnp.where(me == slab - 1, above, high)
    return back + coupled[None] * low[:, None] + tail[None] * high[:, None]


def solution(mesh):
    in_specs = (
        P("mode", "depth", None, None),
        P("depth", None, None),
        P(None, "depth", None, None),
        P("depth", None, None),
        P(),
        P(),
        P(),
    )
    out_specs = P("mode", "depth", None, None)
    return jax.shard_map(local, mesh=mesh, in_specs=in_specs, out_specs=out_specs, check_vma=False)
```

```python
import jax
import jax.numpy as jnp
from jax import lax
from jax.experimental import pallas as pl
from jax.experimental.pallas import tpu as pltpu
from jax.sharding import PartitionSpec as P


def neighbour_masks(shape, axis):
    size = shape[axis]
    where_from = lax.broadcasted_iota(jnp.int32, shape, axis)
    return [
        (shift, jnp.abs(pltpu.roll(where_from, shift, axis) - where_from) == 1)
        for shift in (1, size - 1)
    ]


def stencil_kernel(fields_ref, out_ref):
    rows = fields_ref.shape[1]
    plane = fields_ref.shape[2:]
    masks = neighbour_masks(plane, 0) + neighbour_masks(plane, 1)
    axes = [0, 0, 1, 1]
    for z in range(rows):
        centre = fields_ref[0, z]
        beside = jnp.zeros_like(centre)
        if z + 1 < rows:
            beside = beside + fields_ref[0, z + 1]
        if z > 0:
            beside = beside + fields_ref[0, z - 1]
        for axis, (shift, inside) in zip(axes, masks):
            beside = beside + jnp.where(inside, pltpu.roll(centre, shift, axis), 0.0)
        out_ref[z, 0] = 6.0 * centre - beside


def slab_stencil(fields):
    modes, rows = fields.shape[0], fields.shape[1]
    plane = fields.shape[2:]
    return pl.pallas_call(
        stencil_kernel,
        grid=(modes,),
        in_specs=[pl.BlockSpec((1, rows) + plane, lambda i: (i, 0, 0, 0))],
        out_specs=pl.BlockSpec((rows, 1) + plane, lambda i: (0, i, 0, 0)),
        out_shape=jax.ShapeDtypeStruct((rows, modes) + plane, jnp.float32),
    )(fields)


def edge_kernel(stencil_ref, below_ref, above_ref, out_ref):
    halo = jnp.where(pl.program_id(0) == 0, below_ref[...], above_ref[...])
    out_ref[...] = stencil_ref[...] - halo[None]


def add_edges(stencil, below, above):
    rows = stencil.shape[0]
    edge = (1,) + stencil.shape[1:]
    at_edge = lambda i: (i * (rows - 1), 0, 0, 0)
    return pl.pallas_call(
        edge_kernel,
        grid=(2,),
        in_specs=[
            pl.BlockSpec(edge, at_edge),
            pl.BlockSpec(below.shape, lambda i: (0, 0, 0)),
            pl.BlockSpec(above.shape, lambda i: (0, 0, 0)),
        ],
        out_specs=pl.BlockSpec(edge, at_edge),
        out_shape=jax.ShapeDtypeStruct(stencil.shape, jnp.float32),
        input_output_aliases={0: 0},
    )(stencil, below, above)


def decay_kernel(decay_ref, coupled_ref, tail_ref):
    rows = decay_ref.shape[0]
    lateral = decay_ref.shape[1:]

    def forward_row(z, ratio):
        d = decay_ref[z]
        ratio = d * ratio
        coupled_ref[z] = jnp.sqrt(1.0 - d * d) * ratio
        return ratio

    lax.fori_loop(0, rows, forward_row, jnp.ones(lateral, jnp.float32), unroll=True)

    def backward_row(i, carried):
        z = rows - 1 - i
        coupled, tail = carried
        d = decay_ref[z]
        coupled = d * coupled + coupled_ref[z]
        tail = d * tail
        coupled_ref[z] = coupled
        tail_ref[z] = tail
        return coupled, tail

    lax.fori_loop(
        0,
        rows,
        backward_row,
        (jnp.zeros(lateral, jnp.float32), jnp.ones(lateral, jnp.float32)),
        unroll=True,
    )


def decay_weights(decay):
    return pl.pallas_call(
        decay_kernel,
        out_shape=(
            jax.ShapeDtypeStruct(decay.shape, jnp.float32),
            jax.ShapeDtypeStruct(decay.shape, jnp.float32),
        ),
    )(decay)


def sweep_kernel(mixed_ref, decay_ref, coupled_ref, tail_ref, back_ref, summary_ref):
    rows = decay_ref.shape[0]
    chunk = mixed_ref.shape[2]
    lateral = decay_ref.shape[1:]
    modes = mixed_ref.shape[1]

    def forward_row(z, state):
        d = decay_ref[z]
        g = jnp.sqrt(1.0 - d * d)
        state = d[None] * state + g[None] * mixed_ref[z // chunk, :, z % chunk]
        back_ref[:, z] = g[None] * state
        return state

    state = lax.fori_loop(
        0, rows, forward_row, jnp.zeros((modes,) + lateral, jnp.float32), unroll=True
    )

    def backward_row(i, back):
        z = rows - 1 - i
        back = decay_ref[z][None] * back + back_ref[:, z]
        back_ref[:, z] = back
        return back

    back = lax.fori_loop(
        0, rows, backward_row, jnp.zeros((modes,) + lateral, jnp.float32), unroll=True
    )
    for copy in range(summary_ref.shape[0]):
        summary_ref[copy, 0] = tail_ref[0]
        summary_ref[copy, 1] = coupled_ref[0]
        summary_ref[copy, 2 : 2 + modes] = state
        summary_ref[copy, 2 + modes :] = back


def local_sweeps(mixed, decay, coupled, tail, copies):
    groups, modes, chunk = mixed.shape[0], mixed.shape[1], mixed.shape[2]
    rows = decay.shape[0]
    lateral = decay.shape[1:]
    parts = 2
    half = (lateral[0] // parts, lateral[1])
    by_row = pl.BlockSpec((rows,) + half, lambda i: (0, i, 0))
    return pl.pallas_call(
        sweep_kernel,
        grid=(parts,),
        in_specs=[
            pl.BlockSpec((groups, modes, chunk) + half, lambda i: (0, 0, 0, i, 0)),
            by_row,
            by_row,
            by_row,
        ],
        out_specs=(
            pl.BlockSpec((modes, rows) + half, lambda i: (0, 0, i, 0)),
            pl.BlockSpec((copies, 2 + 2 * modes) + half, lambda i: (0, 0, i, 0)),
        ),
        out_shape=(
            jax.ShapeDtypeStruct((modes, rows) + lateral, jnp.float32),
            jax.ShapeDtypeStruct((copies, 2 + 2 * modes) + lateral, jnp.float32),
        ),
    )(mixed, decay, coupled, tail)


def local(fields, mean_field, kl_modes, decay, coupling, pattern, mode_order):
    local_modes = fields.shape[0]
    rows = fields.shape[1]
    lateral = fields.shape[2:]
    mode_total = mode_order.shape[0]
    groups = lax.axis_size("mode")
    chunk = rows // groups
    masked = coupling * pattern.astype(jnp.float32)
    coupling_table = jnp.take(jnp.take(masked, mode_order, axis=0), mode_order, axis=1)
    term_total = coupling_table.shape[2]

    slabs = lax.axis_size("depth")
    from_below = lax.ppermute(fields[:, -1], "depth", [(i, i + 1) for i in range(slabs - 1)])
    from_above = lax.ppermute(fields[:, 0], "depth", [(i + 1, i) for i in range(slabs - 1)])
    stencil = add_edges(slab_stencil(fields), from_below, from_above)
    stencil = jnp.transpose(stencil, (1, 0, 2, 3))
    stencil_rows = lax.all_to_all(stencil, "mode", 1, 0, tiled=True)
    cell_count = chunk * lateral[0] * lateral[1]
    stencil_rows = stencil_rows.reshape(mode_total, cell_count)

    coefficients = jnp.concatenate([mean_field[None], kl_modes], axis=0)
    my_chunk = lax.axis_index("mode") * chunk
    coefficients = lax.dynamic_slice_in_dim(coefficients, my_chunk, chunk, axis=1)
    coefficients = coefficients.reshape(term_total, 1, cell_count)

    table_rows = jnp.transpose(coupling_table, (2, 0, 1)).reshape(term_total * mode_total, mode_total)
    accumulated = jnp.dot(
        table_rows,
        stencil_rows,
        precision=lax.Precision.HIGH,
        preferred_element_type=jnp.float32,
    ).reshape(term_total, mode_total, cell_count)
    mixed_rows = jnp.sum(coefficients * accumulated, axis=0)
    mixed_rows = mixed_rows.reshape((mode_total, chunk) + lateral)
    mixed_field = lax.all_to_all(mixed_rows, "mode", 0, 0, tiled=True)
    mixed_field = mixed_field.reshape((groups, local_modes, chunk) + lateral)

    coupled, tail = decay_weights(decay)
    back, copies = local_sweeps(mixed_field, decay, coupled, tail, slabs)
    summaries = lax.all_to_all(copies, "depth", 0, 0, tiled=True)
    ratio_all = summaries[:, 0]
    coupled_all = summaries[:, 1]
    forward_all = summaries[:, 2 : 2 + local_modes]
    back_all = summaries[:, 2 + local_modes :]

    me = lax.axis_index("depth")
    entering = [jnp.zeros_like(forward_all[0])]
    for slab in range(slabs - 1):
        entering.append(ratio_all[slab][None] * entering[-1] + forward_all[slab])
    low = entering[0]
    for slab in range(1, slabs):
        low = jnp.where(me == slab, entering[slab], low)
    above = jnp.zeros_like(forward_all[0])
    high = above
    for slab in range(slabs - 1, 0, -1):
        above = (
            back_all[slab]
            + coupled_all[slab][None] * entering[slab]
            + ratio_all[slab][None] * above
        )
        high = jnp.where(me == slab - 1, above, high)
    return back + coupled[None] * low[:, None] + tail[None] * high[:, None]


def solution(mesh):
    in_specs = (
        P("mode", "depth", None, None),
        P("depth", None, None),
        P(None, "depth", None, None),
        P("depth", None, None),
        P(),
        P(),
        P(),
    )
    out_specs = P("mode", "depth", None, None)
    return jax.shard_map(local, mesh=mesh, in_specs=in_specs, out_specs=out_specs, check_vma=False)
```

```python
import jax
import jax.numpy as jnp
from jax import lax
from jax.experimental import pallas as pl
from jax.experimental.pallas import tpu as pltpu
from jax.sharding import PartitionSpec as P


def neighbour_masks(shape, axis):
    size = shape[axis]
    where_from = lax.broadcasted_iota(jnp.int32, shape, axis)
    return [
        (shift, jnp.abs(pltpu.roll(where_from, shift, axis) - where_from) == 1)
        for shift in (1, size - 1)
    ]


def stencil_kernel(fields_ref, out_ref):
    rows = fields_ref.shape[1]
    plane = fields_ref.shape[2:]
    masks = neighbour_masks(plane, 0) + neighbour_masks(plane, 1)
    axes = [0, 0, 1, 1]
    for z in range(rows):
        centre = fields_ref[0, z]
        beside = jnp.zeros_like(centre)
        if z + 1 < rows:
            beside = beside + fields_ref[0, z + 1]
        if z > 0:
            beside = beside + fields_ref[0, z - 1]
        for axis, (shift, inside) in zip(axes, masks):
            beside = beside + jnp.where(inside, pltpu.roll(centre, shift, axis), 0.0)
        out_ref[z, 0] = 6.0 * centre - beside


def slab_stencil(fields):
    modes, rows = fields.shape[0], fields.shape[1]
    plane = fields.shape[2:]
    return pl.pallas_call(
        stencil_kernel,
        grid=(modes,),
        in_specs=[pl.BlockSpec((1, rows) + plane, lambda i: (i, 0, 0, 0))],
        out_specs=pl.BlockSpec((rows, 1) + plane, lambda i: (0, i, 0, 0)),
        out_shape=jax.ShapeDtypeStruct((rows, modes) + plane, jnp.float32),
    )(fields)


def edge_kernel(stencil_ref, below_ref, above_ref, out_ref):
    halo = jnp.where(pl.program_id(0) == 0, below_ref[...], above_ref[...])
    out_ref[...] = stencil_ref[...] - halo[None]


def add_edges(stencil, below, above):
    rows = stencil.shape[0]
    edge = (1,) + stencil.shape[1:]
    at_edge = lambda i: (i * (rows - 1), 0, 0, 0)
    return pl.pallas_call(
        edge_kernel,
        grid=(2,),
        in_specs=[
            pl.BlockSpec(edge, at_edge),
            pl.BlockSpec(below.shape, lambda i: (0, 0, 0)),
            pl.BlockSpec(above.shape, lambda i: (0, 0, 0)),
        ],
        out_specs=pl.BlockSpec(edge, at_edge),
        out_shape=jax.ShapeDtypeStruct(stencil.shape, jnp.float32),
        input_output_aliases={0: 0},
    )(stencil, below, above)


def sweep_kernel(mixed_ref, decay_ref, back_ref, coupled_ref, tail_ref, summary_ref):
    rows = decay_ref.shape[0]
    chunk = mixed_ref.shape[2]

    def forward_row(z, carried):
        state, ratio = carried
        d = decay_ref[z]
        g = jnp.sqrt(1.0 - d * d)
        state = d[None] * state + g[None] * mixed_ref[z // chunk, :, z % chunk]
        ratio = d * ratio
        back_ref[:, z] = g[None] * state
        coupled_ref[z] = g * ratio
        return state, ratio

    lateral = decay_ref.shape[1:]
    modes = mixed_ref.shape[1]
    state, _ = lax.fori_loop(
        0,
        rows,
        forward_row,
        (jnp.zeros((modes,) + lateral, jnp.float32), jnp.ones(lateral, jnp.float32)),
        unroll=True,
    )

    def backward_row(i, carried):
        z = rows - 1 - i
        back, coupled, tail = carried
        d = decay_ref[z]
        back = d[None] * back + back_ref[:, z]
        coupled = d * coupled + coupled_ref[z]
        tail = d * tail
        back_ref[:, z] = back
        coupled_ref[z] = coupled
        tail_ref[z] = tail
        return back, coupled, tail

    back, coupled, tail = lax.fori_loop(
        0,
        rows,
        backward_row,
        (
            jnp.zeros((modes,) + lateral, jnp.float32),
            jnp.zeros(lateral, jnp.float32),
            jnp.ones(lateral, jnp.float32),
        ),
        unroll=True,
    )
    for copy in range(summary_ref.shape[0]):
        summary_ref[copy, 0] = tail
        summary_ref[copy, 1] = coupled
        summary_ref[copy, 2 : 2 + modes] = state
        summary_ref[copy, 2 + modes :] = back


def local_sweeps(mixed, decay, copies):
    groups, modes, chunk = mixed.shape[0], mixed.shape[1], mixed.shape[2]
    rows = decay.shape[0]
    lateral = decay.shape[1:]
    parts = 1
    half = (lateral[0] // parts, lateral[1])
    return pl.pallas_call(
        sweep_kernel,
        grid=(parts,),
        in_specs=[
            pl.BlockSpec((groups, modes, chunk) + half, lambda i: (0, 0, 0, i, 0)),
            pl.BlockSpec((rows,) + half, lambda i: (0, i, 0)),
        ],
        out_specs=(
            pl.BlockSpec((modes, rows) + half, lambda i: (0, 0, i, 0)),
            pl.BlockSpec((rows,) + half, lambda i: (0, i, 0)),
            pl.BlockSpec((rows,) + half, lambda i: (0, i, 0)),
            pl.BlockSpec((copies, 2 + 2 * modes) + half, lambda i: (0, 0, i, 0)),
        ),
        out_shape=(
            jax.ShapeDtypeStruct((modes, rows) + lateral, jnp.float32),
            jax.ShapeDtypeStruct(decay.shape, jnp.float32),
            jax.ShapeDtypeStruct(decay.shape, jnp.float32),
            jax.ShapeDtypeStruct((copies, 2 + 2 * modes) + lateral, jnp.float32),
        ),
    )(mixed, decay)


def local(fields, mean_field, kl_modes, decay, coupling, pattern, mode_order):
    local_modes = fields.shape[0]
    rows = fields.shape[1]
    lateral = fields.shape[2:]
    mode_total = mode_order.shape[0]
    groups = lax.axis_size("mode")
    chunk = rows // groups
    masked = coupling * pattern.astype(jnp.float32)
    coupling_table = jnp.take(jnp.take(masked, mode_order, axis=0), mode_order, axis=1)
    term_total = coupling_table.shape[2]

    slabs = lax.axis_size("depth")
    from_below = lax.ppermute(fields[:, -1], "depth", [(i, i + 1) for i in range(slabs - 1)])
    from_above = lax.ppermute(fields[:, 0], "depth", [(i + 1, i) for i in range(slabs - 1)])
    stencil = add_edges(slab_stencil(fields), from_below, from_above)
    stencil = jnp.transpose(stencil, (1, 0, 2, 3))
    stencil_rows = lax.all_to_all(stencil, "mode", 1, 0, tiled=True)
    cell_count = chunk * lateral[0] * lateral[1]
    stencil_rows = stencil_rows.reshape(mode_total, cell_count)

    coefficients = jnp.concatenate([mean_field[None], kl_modes], axis=0)
    my_chunk = lax.axis_index("mode") * chunk
    coefficients = lax.dynamic_slice_in_dim(coefficients, my_chunk, chunk, axis=1)
    coefficients = coefficients.reshape(term_total, 1, cell_count)

    table_rows = jnp.transpose(coupling_table, (2, 0, 1)).reshape(term_total * mode_total, mode_total)
    accumulated = jnp.dot(
        table_rows,
        stencil_rows,
        precision=lax.Precision.HIGH,
        preferred_element_type=jnp.float32,
    ).reshape(term_total, mode_total, cell_count)
    mixed_rows = jnp.sum(coefficients * accumulated, axis=0)
    mixed_rows = mixed_rows.reshape((mode_total, chunk) + lateral)
    mixed_field = lax.all_to_all(mixed_rows, "mode", 0, 0, tiled=True)
    mixed_field = mixed_field.reshape((groups, local_modes, chunk) + lateral)

    back, coupled, tail, copies = local_sweeps(mixed_field, decay, slabs)
    summaries = lax.all_to_all(copies, "depth", 0, 0, tiled=True)
    ratio_all = summaries[:, 0]
    coupled_all = summaries[:, 1]
    forward_all = summaries[:, 2 : 2 + local_modes]
    back_all = summaries[:, 2 + local_modes :]

    me = lax.axis_index("depth")
    entering = [jnp.zeros_like(forward_all[0])]
    for slab in range(slabs - 1):
        entering.append(ratio_all[slab][None] * entering[-1] + forward_all[slab])
    low = entering[0]
    for slab in range(1, slabs):
        low = jnp.where(me == slab, entering[slab], low)
    above = jnp.zeros_like(forward_all[0])
    high = above
    for slab in range(slabs - 1, 0, -1):
        above = (
            back_all[slab]
            + coupled_all[slab][None] * entering[slab]
            + ratio_all[slab][None] * above
        )
        high = jnp.where(me == slab - 1, above, high)
    return back + coupled[None] * low[:, None] + tail[None] * high[:, None]


def solution(mesh):
    in_specs = (
        P("mode", "depth", None, None),
        P("depth", None, None),
        P(None, "depth", None, None),
        P("depth", None, None),
        P(),
        P(),
        P(),
    )
    out_specs = P("mode", "depth", None, None)
    return jax.shard_map(local, mesh=mesh, in_specs=in_specs, out_specs=out_specs, check_vma=False)
```
